32 devices in a mesh: row: 4 (over y, core), col: 8 (over z, x).
Axes of the slice: x: 2, y: 2, z: 4, core: 2. Of those that a mesh axis runs over, the one named last changes fastest.
Arguments:
- hess: bfloat16 [10, 4, 256, 5, 8, 256], P(None, 'row', None, None, 'col'), may hold values from -6 to 6
- coupling: float32 [32, 256, 2, 256], P(('row', 'col')), may hold values from -6 to 6
- dest_row: int32 [32, 256, 1], P(('row', 'col')), may hold values from 0 to 3, as said below
- local_row: int32 [32, 256], P(('row', 'col')), may hold values from 256 to 2559
- live: int32 [32], P(('row', 'col')), may hold values from 1 to 256, 6144 in all
- pattern: int32 [40, 40], replicated, may hold values 0 or 1
Outputs:
- factor: float32 [10, 4, 256, 5, 8, 256], P(None, 'row', None, None, 'col')
The draws below stay inside these ranges and needn't reach their ends.
Inputs may be any that keep to these rules, and one draw needn't show every extreme that they name: `dest_row`: among one owner's 256 slots, used or not, one grid row is named exactly 64 times and no grid row more than 64 times. The first live[d] slots of owner d are used; the counts sum to 6144 and one owner uses all 256.
All inputs are finite; a program needn't handle non-finite values. No bound on the sum of `live` on one device may be relied on, other than what follows from the above.
Results may differ from the reference program's by a relative error of at most 0.0003.
Values sent between devices are 32-bit elements; how exact they have to be, the bound alone decides.
No kernel may reach another device: no remote copies, remote signals or barrier semaphores. Data moves between devices by JAX's collectives and lax.ppermute only.
A program may use at most 192 MiB of HBM per device.

```python
import math
import jax
import jax.numpy as jnp
import numpy as np
from jax import lax

B = 256
RB_DEV = 10
SLOTS = 256
NBLK = 40
CB_DEV = 5
OWNERS = 32
CAP = 64
N_ROW = 4
N_COL = 8


def draw_hess(key, part):
    shape = (RB_DEV, N_ROW, B, CB_DEV, N_COL, B)
    base_key = jax.random.fold_in(key, 11)
    noise = jax.random.normal(base_key, shape, jnp.float32)
    values = 1.5 + 0.5 * noise
    values = jnp.clip(values, -6.0, 6.0)
    return values.astype(jnp.bfloat16)


def owner_routes(owner_key):
    keys = jax.random.split(owner_key, 4)
    first_pick = jax.random.randint(keys[0], (), 0, N_ROW, dtype=jnp.int32)
    second_pick = jax.random.randint(keys[1], (), 0, N_ROW, dtype=jnp.int32)
    heavy = jnp.minimum(first_pick, second_pick)
    others = jnp.arange((N_ROW - 1) * CAP, dtype=jnp.int32) // CAP
    others = others + (others >= heavy).astype(jnp.int32)
    shuffled = jax.random.permutation(keys[2], others)
    chosen = shuffled[:SLOTS - CAP]
    combined = jnp.concatenate([jnp.zeros((CAP,), jnp.int32) + heavy, chosen], 0)
    return jax.random.permutation(keys[3], combined)


def draw_dest_row(key, part):
    owner_keys = jax.random.split(jax.random.fold_in(key, 7), OWNERS)
    routes_all = jax.vmap(owner_routes)(owner_keys)
    return routes_all[:, :, None].astype(jnp.int32)


def set_ends(values, stream_key, low, largest):
    longest = values.shape.index(max(values.shape))
    spots = []
    for shift in (0, 1):
        where = [jax.random.randint(jax.random.fold_in(stream_key, axis), (), 0, length) for axis, length in enumerate(values.shape)]
        where[longest] = (where[longest] + shift) % values.shape[longest]
        spots.append(tuple(where))
    return values.at[spots[0]].set(low).at[spots[1]].set(largest)


def block_levels(own_key, extent, cuts, least, largest):
    gain, own = 1.0, jax.random.fold_in(own_key, 6)
    for position, blocks in cuts:
        steps = jnp.exp(jax.random.uniform(jax.random.fold_in(own, position), (blocks,), jnp.float32, least / len(cuts), largest / len(cuts)))
        gain = gain * jnp.repeat(steps, extent[position] // blocks).reshape([-1 if axis == position else 1 for axis in range(len(extent))])
    return gain


def split_up(count, total, most, slope):
    weights = [(1 << 20) // math.isqrt(grade ** slope) + 1 for grade in range(2, count + 1)]
    spare, counts = total - most - (count - 1), [1] * (count - 1)
    while spare > 0:
        candidates = [i for i in range(count - 1) if counts[i] < most]
        pool, remaining = sum([weights[i] for i in candidates]), spare
        for i in candidates:
            more = min(most - counts[i], max(1, remaining * weights[i] // pool), spare)
            counts[i] = counts[i] + more
            spare = spare - more
    return np.array([most] + counts)


def ragged_sizes(stream_key, number_of, total, reach, slope):
    if number_of == 2:
        one = jax.random.randint(stream_key, (), max(1, total - reach), min(reach, total - 1) + 1)
        return jnp.stack([one, total - one])
    lengths = jnp.asarray(split_up(number_of, total, reach, slope), jnp.int32)
    twos = (number_of - 1) // 2
    donor, sink = lengths[1:1 + 2 * twos:2], lengths[2:2 + 2 * twos:2]
    slack = jnp.minimum(donor - 1, reach - sink)
    passed = jax.random.randint(jax.random.fold_in(stream_key, 1), (twos,), 0, 1 << 20) % (slack + 1)
    lengths = lengths.at[1:1 + 2 * twos:2].set(donor - passed).at[2:2 + 2 * twos:2].set(sink + passed)
    return lengths[jax.random.permutation(jax.random.fold_in(stream_key, 2), number_of)]


def gaussian(key, extent, width, most, pieces=(), kind=jnp.bfloat16):
    gain = block_levels(key, extent, pieces, -0.22, 0.18) if pieces else 1.0
    values = jax.random.normal(key, extent, jnp.float32) * width * gain
    return jnp.minimum(jnp.maximum(values, -most), most).astype(kind)


def setup_inputs(seed: int = 0) -> dict:
    key_of = jax.random.split(jax.random.key(seed), 7)
    return {
        "hess": draw_hess(jax.random.fold_in(key_of[6], 71), 0),
        "coupling": gaussian(key_of[1], (OWNERS, SLOTS, 2, B), 1.0, 6.0, ((0, 32),), jnp.float32),
        "dest_row": draw_dest_row(jax.random.fold_in(key_of[6], 71), 0),
        "local_row": set_ends(jax.random.randint(key_of[3], (OWNERS, SLOTS), B, RB_DEV * B), jax.random.fold_in(key_of[3], 1), B, (RB_DEV * B) - 1).astype(jnp.int32),
        "live": ragged_sizes(key_of[4], OWNERS, OWNERS * SLOTS * 3 // 4, SLOTS, 2).astype(jnp.int32),
        "pattern": set_ends((jax.random.randint(key_of[5], (NBLK, NBLK), 0, 2) < 1).astype(jnp.int32), jax.random.fold_in(key_of[5], 1), 0, 1),
    }


def symmetric(block):
    return jnp.tril(block) + jnp.swapaxes(jnp.tril(block, -1), -1, -2)

def right_solve(rows, lower_factor):
    return jax.scipy.linalg.solve_triangular(lower_factor, rows.T, lower=True).T

def leading(block00, block10, block11, link):
    size = block00.shape[0]
    first = symmetric(block00)
    second = symmetric(block11)
    coupled = link * block10
    whole = jnp.concatenate([jnp.concatenate([first, coupled.T], 1), jnp.concatenate([coupled, second], 1)], 0)
    ident = jnp.eye(2 * size, dtype=whole.dtype)
    spread = jnp.sum(jnp.abs(whole), axis=1) - jnp.abs(jnp.diagonal(whole))
    whole = whole * (1.0 - ident) + ident * (1.0 + spread)[:, None]
    factor00 = jnp.linalg.cholesky(whole[:size, :size])
    factor10 = right_solve(whole[size:, :size], factor00)
    reduced = whole[size:, size:] - jnp.dot(factor10, factor10.T, precision=lax.Precision.HIGHEST)
    factor11 = jnp.linalg.cholesky(reduced)
    return (factor00, factor10, factor11)

def reference(hess, coupling, dest_row, local_row, live, pattern):
    order = NBLK * B
    matrix = hess.astype(jnp.float32).reshape(order, order)
    blocks = matrix.reshape(NBLK, B, NBLK, B)
    mask = pattern.astype(jnp.float32)
    slot_ids = jnp.arange(SLOTS, dtype=jnp.int32)
    active = slot_ids[None, :] < live[:, None]
    target = (local_row // B * N_ROW + dest_row[:, :, 0]) * B + local_row % B
    moved = jnp.where(active[:, :, None, None], coupling, 0.0)
    extra = jnp.zeros((order, 2, B), jnp.float32).at[target.reshape(-1)].add(moved.reshape(-1, 2, B))
    panel = jnp.stack([matrix[:, :B], matrix[:, B:2 * B]], 1) + extra
    rowmask = jnp.repeat(mask[:, :2], B, axis=0)
    panel = panel * rowmask[:, :, None]
    f00, f10, f11 = leading(blocks[0, :, 0], blocks[1, :, 0], blocks[1, :, 1], mask[1, 0])
    first = right_solve(panel[:, 0], f00)
    second = right_solve(panel[:, 1] - jnp.dot(first, f10.T, precision=lax.Precision.HIGHEST), f11)
    empty = jnp.zeros((B, B), jnp.float32)
    first = jnp.concatenate([f00, f10, first[2 * B:]], 0)
    second = jnp.concatenate([empty, f11, second[2 * B:]], 0)
    factor = jnp.concatenate([first, second], 1)
    index = jnp.arange(NBLK, dtype=jnp.int32)
    filler = jnp.zeros((NBLK - 2, B, B), jnp.float32)

    def row_block(i):
        rows = lax.dynamic_slice_in_dim(matrix, i * B, B, 0)
        left = lax.dynamic_slice_in_dim(factor, i * B, B, 0)
        update = jnp.dot(left, factor.T, precision=lax.Precision.HIGHEST)
        tiles = jnp.swapaxes(rows.reshape(B, NBLK, B), 0, 1)
        sym = symmetric(tiles)
        links = lax.dynamic_index_in_dim(mask, i, 0, keepdims=False)
        base = jnp.where((index == i)[:, None, None], sym, jnp.where((index < i)[:, None, None], links[:, None, None] * tiles, 0.0))
        trail = base - jnp.swapaxes(update.reshape(B, NBLK, B), 0, 1)
        panel_part = jnp.concatenate([jnp.swapaxes(left.reshape(B, 2, B), 0, 1), filler], 0)
        result = jnp.where((index < 2)[:, None, None], panel_part, jnp.where((index <= i)[:, None, None], trail, 0.0))
        return jnp.swapaxes(result, 0, 1).reshape(B, order)
    full = lax.map(row_block, index).reshape(order, order)
    return full.reshape(RB_DEV, N_ROW, B, CB_DEV, N_COL, B)
```

```python
import jax
import jax.numpy as jnp
from jax import lax
from jax.sharding import PartitionSpec as P

HIGH = lax.Precision.HIGHEST


def symmetric(block):
    return jnp.tril(block) + jnp.swapaxes(jnp.tril(block, -1), -1, -2)


def lower_inverse(lower_factor):
    ident = jnp.eye(lower_factor.shape[0], dtype=lower_factor.dtype)
    return jax.scipy.linalg.solve_triangular(lower_factor, ident, lower=True)


def leading(block00, block10, block11, link):
    size = block00.shape[0]
    first = symmetric(block00)
    second = symmetric(block11)
    coupled = link * block10
    whole = jnp.concatenate(
        [jnp.concatenate([first, coupled.T], 1), jnp.concatenate([coupled, second], 1)], 0
    )
    ident = jnp.eye(2 * size, dtype=whole.dtype)
    spread = jnp.sum(jnp.abs(whole), axis=1) - jnp.abs(jnp.diagonal(whole))
    whole = whole * (1.0 - ident) + ident * (1.0 + spread)[:, None]
    factor00 = jnp.linalg.cholesky(whole[:size, :size])
    inv00 = lower_inverse(factor00)
    factor10 = jnp.dot(whole[size:, :size], inv00.T, precision=HIGH)
    reduced = whole[size:, size:] - jnp.dot(factor10, factor10.T, precision=HIGH)
    factor11 = jnp.linalg.cholesky(reduced)
    inv11 = lower_inverse(factor11)
    return factor00, factor10, factor11, inv00, inv11


def shards(hess, coupling, dest_row, local_row, live, pattern):
    grid_rows = lax.axis_size("row")
    grid_cols = lax.axis_size("col")
    here_row = lax.axis_index("row")
    here_col = lax.axis_index("col")
    row_blocks = hess.shape[0]
    col_blocks = hess.shape[3]
    block = hess.shape[2]
    slot_count = coupling.shape[1]
    bucket = slot_count // 4
    height = row_blocks * block
    width = col_blocks * block
    ratio = grid_cols // grid_rows
    mask = pattern.astype(jnp.float32)

    corner = hess[0, 0, :, 0, 0, :].astype(jnp.float32)
    at_first = ((here_row == 0) & (here_col == 0)).astype(jnp.float32)
    at_below = ((here_row == 1) & (here_col == 0)).astype(jnp.float32)
    at_second = ((here_row == 1) & (here_col == 1)).astype(jnp.float32)
    pivots = lax.psum(
        jnp.stack([at_first * corner, at_below * corner, at_second * corner]), ("row", "col")
    )

    grid_ids = jnp.arange(grid_rows, dtype=jnp.int32)
    dest = dest_row[0, :, 0]
    active = jnp.arange(slot_count, dtype=jnp.int32) < live[0]
    hits = (dest[:, None] == grid_ids[None, :]) & active[:, None]
    ranks = jnp.cumsum(hits.astype(jnp.int32), axis=0) - 1
    place = jnp.sum(jnp.where(hits, ranks + grid_ids[None, :] * bucket, 0), axis=1)
    place = jnp.where(active, place, -1)
    pick = jnp.arange(grid_rows * bucket, dtype=jnp.int32)[:, None] == place[None, :]
    outgoing = jnp.dot(
        pick.astype(jnp.float32), coupling[0].reshape(slot_count, 2 * block), precision=HIGH
    )
    labels = jnp.sum(jnp.where(pick, local_row[0][None, :], 0), axis=1).astype(jnp.float32)
    arrived = lax.all_to_all(
        outgoing.reshape(grid_rows, bucket, 2 * block), "row", split_axis=0, concat_axis=0, tiled=True
    )
    arrived_rows = lax.all_to_all(
        labels.reshape(grid_rows, bucket), "row", split_axis=0, concat_axis=0, tiled=True
    )
    spots = arrived_rows.reshape(-1).astype(jnp.int32)
    spread = jnp.arange(height, dtype=jnp.int32)[:, None] == spots[None, :]
    partial_value = jnp.dot(
        spread.astype(jnp.float32), arrived.reshape(-1, 2 * block), precision=HIGH
    ).reshape(height, 2, block)
    own = hess[:, 0, :, 0, 0, :].astype(jnp.float32).reshape(height, block)
    which = (jnp.arange(2, dtype=jnp.int32) == here_col).astype(jnp.float32)
    partial_value = partial_value + own[:, None, :] * which[None, :, None]

    f00, f10, f11, inv00, inv11 = leading(pivots[0], pivots[1], pivots[2], mask[1, 0])

    mine = lax.dynamic_index_in_dim(
        mask.reshape(row_blocks, grid_rows, -1), here_row, 1, keepdims=False
    )
    rowmask = jnp.repeat(mine[:, :2], block, axis=0)
    summed = lax.psum(partial_value, "col") * rowmask[:, :, None]
    first = jnp.dot(summed[:, 0], inv00.T, precision=HIGH)
    second = jnp.dot(
        summed[:, 1] - jnp.dot(first, f10.T, precision=HIGH), inv11.T, precision=HIGH
    )
    panel = jnp.stack([first, second], 1)
    head_first = jnp.where(here_row == 0, f00, f10)
    head_second = jnp.where(here_row == 0, jnp.zeros_like(f11), f11)
    head = jnp.stack([head_first, head_second], 1)
    panel = panel.at[:block].set(jnp.where(here_row < 2, head, panel[:block]))

    picked = lax.dynamic_index_in_dim(
        panel.reshape(col_blocks, ratio, block, 2, block), here_col // grid_rows, 1, keepdims=False
    )
    pairs = []
    for g in range(grid_rows):
        for s in range(grid_cols):
            dst_row = s % grid_rows
            dst_col = g + grid_rows * (s // grid_rows)
            pairs.append((g * grid_cols + s, dst_row * grid_cols + dst_col))
    across = lax.ppermute(picked, ("row", "col"), pairs)

    left = panel.reshape(height, 2 * block)
    right = across.reshape(width, 2 * block)
    update = jnp.dot(left, right.T, precision=HIGH)

    tiles = hess[:, 0, :, :, 0, :].astype(jnp.float32).reshape(height, width)
    block_i = jnp.arange(row_blocks, dtype=jnp.int32) * grid_rows + here_row
    block_j = jnp.arange(col_blocks, dtype=jnp.int32) * grid_cols + here_col
    links = lax.dynamic_index_in_dim(
        lax.dynamic_index_in_dim(
            mask.reshape(row_blocks, grid_rows, col_blocks, grid_cols), here_row, 1, keepdims=False
        ),
        here_col,
        2,
        keepdims=False,
    )
    full_i = jnp.repeat(block_i, block)[:, None]
    full_j = jnp.repeat(block_j, block)[None, :]
    full_links = jnp.repeat(jnp.repeat(links, block, axis=0), block, axis=1)
    result = jnp.where(full_i > full_j, full_links * tiles - update, 0.0)

    on_diag = here_row == here_col % grid_rows
    tri = jnp.arange(block)[:, None] >= jnp.arange(block)[None, :]
    for u in range(col_blocks):
        top = (u * ratio + here_col // grid_rows) * block
        own_tile = lax.dynamic_slice(tiles, (top, u * block), (block, block))
        sym_tile = jnp.where(tri, own_tile, own_tile.T)
        upd_tile = lax.dynamic_slice(update, (top, u * block), (block, block))
        old_tile = lax.dynamic_slice(result, (top, u * block), (block, block))
        new_tile = jnp.where(on_diag, sym_tile - upd_tile, old_tile)
        result = lax.dynamic_update_slice(result, new_tile, (top, u * block))

    panel_col = lax.dynamic_index_in_dim(panel, jnp.minimum(here_col, 1), 1, keepdims=False)
    result = result.at[:, :block].set(jnp.where(here_col < 2, panel_col, result[:, :block]))
    return result.reshape(row_blocks, 1, block, col_blocks, 1, block)


def solution(mesh):
    return jax.shard_map(
        shards,
        mesh=mesh,
        in_specs=(
            P(None, "row", None, None, "col", None),
            P(("row", "col"), None, None, None),
            P(("row", "col"), None, None),
            P(("row", "col"), None),
            P(("row", "col")),
            P(),
        ),
        out_specs=P(None, "row", None, None, "col", None),
        check_vma=False,
    )
```

```python
import jax
import jax.numpy as jnp
from jax import lax
from jax.sharding import PartitionSpec as P

HIGH = lax.Precision.HIGHEST


def symmetric(block):
    return jnp.tril(block) + jnp.swapaxes(jnp.tril(block, -1), -1, -2)


def lower_inverse(lower_factor):
    ident = jnp.eye(lower_factor.shape[0], dtype=lower_factor.dtype)
    return jax.scipy.linalg.solve_triangular(lower_factor, ident, lower=True)


def leading(block00, block10, block11, link):
    size = block00.shape[0]
    first = symmetric(block00)
    second = symmetric(block11)
    coupled = link * block10
    whole = jnp.concatenate(
        [jnp.concatenate([first, coupled.T], 1), jnp.concatenate([coupled, second], 1)], 0
    )
    ident = jnp.eye(2 * size, dtype=whole.dtype)
    spread = jnp.sum(jnp.abs(whole), axis=1) - jnp.abs(jnp.diagonal(whole))
    whole = whole * (1.0 - ident) + ident * (1.0 + spread)[:, None]
    factor00 = jnp.linalg.cholesky(whole[:size, :size])
    inv00 = lower_inverse(factor00)
    factor10 = jnp.dot(whole[size:, :size], inv00.T, precision=HIGH)
    reduced = whole[size:, size:] - jnp.dot(factor10, factor10.T, precision=HIGH)
    factor11 = jnp.linalg.cholesky(reduced)
    inv11 = lower_inverse(factor11)
    return factor00, factor10, factor11, inv00, inv11


def shards(hess, coupling, dest_row, local_row, live, pattern):
    grid_rows = lax.axis_size("row")
    grid_cols = lax.axis_size("col")
    here_row = lax.axis_index("row")
    here_col = lax.axis_index("col")
    row_blocks = hess.shape[0]
    col_blocks = hess.shape[3]
    block = hess.shape[2]
    slot_count = coupling.shape[1]
    bucket = slot_count // 4
    height = row_blocks * block
    width = col_blocks * block
    ratio = grid_cols // grid_rows
    mask = pattern.astype(jnp.float32)

    corner = hess[0, 0, :, 0, 0, :].astype(jnp.float32)
    devices = grid_rows * grid_cols
    here = here_row * grid_cols + here_col
    pivots = []
    for source in (0, grid_cols, grid_cols + 1):
        value = jnp.where(here == source, corner, 0.0)
        reach = 1
        while reach < devices:
            pairs = [
                ((source + m) % devices, (source + m + reach) % devices)
                for m in range(min(reach, devices - reach))
            ]
            value = value + lax.ppermute(value, ("row", "col"), pairs)
            reach *= 2
        pivots.append(value)

    grid_ids = jnp.arange(grid_rows, dtype=jnp.int32)
    dest = dest_row[0, :, 0]
    active = jnp.arange(slot_count, dtype=jnp.int32) < live[0]
    hits = (dest[:, None] == grid_ids[None, :]) & active[:, None]
    ranks = jnp.cumsum(hits.astype(jnp.int32), axis=0) - 1
    place = jnp.sum(jnp.where(hits, ranks + grid_ids[None, :] * bucket, 0), axis=1)
    place = jnp.where(active, place, -1)
    pick = jnp.arange(grid_rows * bucket, dtype=jnp.int32)[:, None] == place[None, :]
    outgoing = jnp.dot(
        pick.astype(jnp.float32), coupling[0].reshape(slot_count, 2 * block), precision=HIGH
    )
    labels = jnp.sum(jnp.where(pick, local_row[0][None, :], 0), axis=1).astype(jnp.float32)
    arrived = lax.all_to_all(
        outgoing.reshape(grid_rows, bucket, 2 * block), "row", split_axis=0, concat_axis=0, tiled=True
    )
    arrived_rows = lax.all_to_all(
        labels.reshape(grid_rows, bucket), "row", split_axis=0, concat_axis=0, tiled=True
    )
    spots = arrived_rows.reshape(-1).astype(jnp.int32)
    spread = jnp.arange(height, dtype=jnp.int32)[:, None] == spots[None, :]
    partial_value = jnp.dot(
        spread.astype(jnp.float32), arrived.reshape(-1, 2 * block), precision=HIGH
    ).reshape(height, 2, block)
    own = hess[:, 0, :, 0, 0, :].astype(jnp.float32).reshape(height, block)
    which = (jnp.arange(2, dtype=jnp.int32) == here_col).astype(jnp.float32)
    partial_value = partial_value + own[:, None, :] * which[None, :, None]

    f00, f10, f11, inv00, inv11 = leading(pivots[0], pivots[1], pivots[2], mask[1, 0])

    mine = lax.dynamic_index_in_dim(
        mask.reshape(row_blocks, grid_rows, -1), here_row, 1, keepdims=False
    )
    rowmask = jnp.repeat(mine[:, :2], block, axis=0)
    chunk = height // grid_cols
    pieces = lax.all_to_all(
        partial_value.reshape(grid_cols, chunk, 2, block), "col", split_axis=0, concat_axis=0, tiled=True
    )
    chunk_mask = lax.dynamic_slice_in_dim(rowmask, here_col * chunk, chunk, 0)
    summed = jnp.sum(pieces, axis=0) * chunk_mask[:, :, None]
    first = jnp.dot(summed[:, 0], inv00.T, precision=HIGH)
    second = jnp.dot(
        summed[:, 1] - jnp.dot(first, f10.T, precision=HIGH), inv11.T, precision=HIGH
    )
    solved = jnp.stack([first, second], 1)
    panel = lax.all_to_all(
        jnp.broadcast_to(solved[None], (grid_cols, chunk, 2, block)),
        "col",
        split_axis=0,
        concat_axis=0,
        tiled=True,
    ).reshape(height, 2, block)
    head_first = jnp.where(here_row == 0, f00, f10)
    head_second = jnp.where(here_row == 0, jnp.zeros_like(f11), f11)
    head = jnp.stack([head_first, head_second], 1)
    panel = panel.at[:block].set(jnp.where(here_row < 2, head, panel[:block]))

    picked = lax.dynamic_index_in_dim(
        panel.reshape(col_blocks, ratio, block, 2, block), here_col // grid_rows, 1, keepdims=False
    )
    pairs = []
    for g in range(grid_rows):
        for s in range(grid_cols):
            dst_row = s % grid_rows
            dst_col = g + grid_rows * (s // grid_rows)
            pairs.append((g * grid_cols + s, dst_row * grid_cols + dst_col))
    across = lax.ppermute(picked, ("row", "col"), pairs)

    left = panel.reshape(height, 2 * block)
    right = across.reshape(width, 2 * block)
    update = jnp.dot(left, right.T, precision=lax.Precision.HIGH)

    tiles = hess[:, 0, :, :, 0, :].astype(jnp.float32).reshape(height, width)
    block_i = jnp.arange(row_blocks, dtype=jnp.int32) * grid_rows + here_row
    block_j = jnp.arange(col_blocks, dtype=jnp.int32) * grid_cols + here_col
    links = lax.dynamic_index_in_dim(
        lax.dynamic_index_in_dim(
            mask.reshape(row_blocks, grid_rows, col_blocks, grid_cols), here_row, 1, keepdims=False
        ),
        here_col,
        2,
        keepdims=False,
    )
    full_i = jnp.repeat(block_i, block)[:, None]
    full_j = jnp.repeat(block_j, block)[None, :]
    full_links = jnp.repeat(jnp.repeat(links, block, axis=0), block, axis=1)
    result = jnp.where(full_i > full_j, full_links * tiles - update, 0.0)

    on_diag = here_row == here_col % grid_rows
    tri = jnp.arange(block)[:, None] >= jnp.arange(block)[None, :]
    for u in range(col_blocks):
        top = (u * ratio + here_col // grid_rows) * block
        own_tile = lax.dynamic_slice(tiles, (top, u * block), (block, block))
        sym_tile = jnp.where(tri, own_tile, own_tile.T)
        upd_tile = lax.dynamic_slice(update, (top, u * block), (block, block))
        old_tile = lax.dynamic_slice(result, (top, u * block), (block, block))
        new_tile = jnp.where(on_diag, sym_tile - upd_tile, old_tile)
        result = lax.dynamic_update_slice(result, new_tile, (top, u * block))

    panel_col = lax.dynamic_index_in_dim(panel, jnp.minimum(here_col, 1), 1, keepdims=False)
    result = result.at[:, :block].set(jnp.where(here_col < 2, panel_col, result[:, :block]))
    return result.reshape(row_blocks, 1, block, col_blocks, 1, block)


def solution(mesh):
    return jax.shard_map(
        shards,
        mesh=mesh,
        in_specs=(
            P(None, "row", None, None, "col", None),
            P(("row", "col"), None, None, None),
            P(("row", "col"), None, None),
            P(("row", "col"), None),
            P(("row", "col")),
            P(),
        ),
        out_specs=P(None, "row", None, None, "col", None),
        check_vma=False,
    )
```

```python
import jax
import jax.numpy as jnp
from jax import lax
from jax.sharding import PartitionSpec as P

HIGH = lax.Precision.HIGHEST


def symmetric(block):
    return jnp.tril(block) + jnp.swapaxes(jnp.tril(block, -1), -1, -2)


def lower_inverse(lower_factor):
    ident = jnp.eye(lower_factor.shape[0], dtype=lower_factor.dtype)
    return jax.scipy.linalg.solve_triangular(lower_factor, ident, lower=True)


def leading(block00, block10, block11, link):
    size = block00.shape[0]
    first = symmetric(block00)
    second = symmetric(block11)
    coupled = link * block10
    whole = jnp.concatenate(
        [jnp.concatenate([first, coupled.T], 1), jnp.concatenate([coupled, second], 1)], 0
    )
    ident = jnp.eye(2 * size, dtype=whole.dtype)
    spread = jnp.sum(jnp.abs(whole), axis=1) - jnp.abs(jnp.diagonal(whole))
    whole = whole * (1.0 - ident) + ident * (1.0 + spread)[:, None]
    factor00 = jnp.linalg.cholesky(whole[:size, :size])
    inv00 = lower_inverse(factor00)
    factor10 = jnp.dot(whole[size:, :size], inv00.T, precision=HIGH)
    reduced = whole[size:, size:] - jnp.dot(factor10, factor10.T, precision=HIGH)
    factor11 = jnp.linalg.cholesky(reduced)
    inv11 = lower_inverse(factor11)
    return factor00, factor10, factor11, inv00, inv11


def shards(hess, coupling, dest_row, local_row, live, pattern):
    grid_rows = lax.axis_size("row")
    grid_cols = lax.axis_size("col")
    here_row = lax.axis_index("row")
    here_col = lax.axis_index("col")
    row_blocks = hess.shape[0]
    col_blocks = hess.shape[3]
    block = hess.shape[2]
    slot_count = coupling.shape[1]
    bucket = slot_count // 4
    height = row_blocks * block
    width = col_blocks * block
    ratio = grid_cols // grid_rows
    mask = pattern.astype(jnp.float32)

    corner = hess[0, 0, :, 0, 0, :].astype(jnp.float32)
    devices = grid_rows * grid_cols
    here = here_row * grid_cols + here_col
    pivots = []
    for source in (0, grid_cols, grid_cols + 1):
        value = jnp.where(here == source, corner, 0.0)
        reach = 1
        while reach < devices:
            pairs = [
                ((source + m) % devices, (source + m + reach) % devices)
                for m in range(min(reach, devices - reach))
            ]
            value = value + lax.ppermute(value, ("row", "col"), pairs)
            reach *= 2
        pivots.append(value)

    grid_ids = jnp.arange(grid_rows, dtype=jnp.int32)
    dest = dest_row[0, :, 0]
    active = jnp.arange(slot_count, dtype=jnp.int32) < live[0]
    hits = (dest[:, None] == grid_ids[None, :]) & active[:, None]
    ranks = jnp.cumsum(hits.astype(jnp.int32), axis=0) - 1
    place = jnp.sum(jnp.where(hits, ranks + grid_ids[None, :] * bucket, 0), axis=1)
    place = jnp.where(active, place, -1)
    pick = jnp.arange(grid_rows * bucket, dtype=jnp.int32)[:, None] == place[None, :]
    outgoing = jnp.dot(
        pick.astype(jnp.float32), coupling[0].reshape(slot_count, 2 * block), precision=HIGH
    )
    labels = jnp.sum(jnp.where(pick, local_row[0][None, :], 0), axis=1).astype(jnp.float32)
    arrived = lax.all_to_all(
        outgoing.reshape(grid_rows, bucket, 2 * block), "row", split_axis=0, concat_axis=0, tiled=True
    )
    arrived_rows = lax.all_to_all(
        labels.reshape(grid_rows, bucket), "row", split_axis=0, concat_axis=0, tiled=True
    )
    spots = arrived_rows.reshape(-1).astype(jnp.int32)
    spread = jnp.arange(height, dtype=jnp.int32)[:, None] == spots[None, :]
    partial_value = jnp.dot(
        spread.astype(jnp.float32), arrived.reshape(-1, 2 * block), precision=HIGH
    ).reshape(height, 2, block)
    own = hess[:, 0, :, 0, 0, :].astype(jnp.float32).reshape(height, block)
    which = (jnp.arange(2, dtype=jnp.int32) == here_col).astype(jnp.float32)
    partial_value = partial_value + own[:, None, :] * which[None, :, None]

    mine = lax.dynamic_index_in_dim(
        mask.reshape(row_blocks, grid_rows, -1), here_row, 1, keepdims=False
    )
    rowmask = jnp.repeat(mine[:, :2], block, axis=0)
    chunk = height // grid_cols
    partial_value, pivots = lax.optimization_barrier((partial_value, pivots))
    pieces = lax.all_to_all(
        partial_value.reshape(grid_cols, chunk, 2, block), "col", split_axis=0, concat_axis=0, tiled=True
    )
    chunk_mask = lax.dynamic_slice_in_dim(rowmask, here_col * chunk, chunk, 0)
    summed = jnp.sum(pieces, axis=0) * chunk_mask[:, :, None]
    assembled = lax.all_to_all(
        jnp.broadcast_to(summed[None], (grid_cols, chunk, 2, block)),
        "col",
        split_axis=0,
        concat_axis=0,
        tiled=True,
    ).reshape(height, 2, block)
    tiles = hess[:, 0, :, :, 0, :].astype(jnp.float32).reshape(height, width)
    block_i = jnp.arange(row_blocks, dtype=jnp.int32) * grid_rows + here_row
    block_j = jnp.arange(col_blocks, dtype=jnp.int32) * grid_cols + here_col
    links = lax.dynamic_index_in_dim(
        lax.dynamic_index_in_dim(
            mask.reshape(row_blocks, grid_rows, col_blocks, grid_cols), here_row, 1, keepdims=False
        ),
        here_col,
        2,
        keepdims=False,
    )
    full_i = jnp.repeat(block_i, block)[:, None]
    full_j = jnp.repeat(block_j, block)[None, :]
    full_links = jnp.repeat(jnp.repeat(links, block, axis=0), block, axis=1)
    base = jnp.where(full_i > full_j, full_links * tiles, 0.0)
    on_diag = here_row == here_col % grid_rows
    tri = jnp.arange(block)[:, None] >= jnp.arange(block)[None, :]
    for u in range(col_blocks):
        top = (u * ratio + here_col // grid_rows) * block
        own_tile = lax.dynamic_slice(tiles, (top, u * block), (block, block))
        sym_tile = jnp.where(tri, own_tile, own_tile.T)
        old_tile = lax.dynamic_slice(base, (top, u * block), (block, block))
        base = lax.dynamic_update_slice(
            base, jnp.where(on_diag, sym_tile, old_tile), (top, u * block)
        )
    base, assembled = lax.optimization_barrier((base, assembled))
    f00, f10, f11, inv00, inv11 = leading(pivots[0], pivots[1], pivots[2], mask[1, 0])
    first = jnp.dot(assembled[:, 0], inv00.T, precision=HIGH)
    second = jnp.dot(
        assembled[:, 1] - jnp.dot(first, f10.T, precision=HIGH), inv11.T, precision=HIGH
    )
    panel = jnp.stack([first, second], 1)
    head_first = jnp.where(here_row == 0, f00, f10)
    head_second = jnp.where(here_row == 0, jnp.zeros_like(f11), f11)
    head = jnp.stack([head_first, head_second], 1)
    panel = panel.at[:block].set(jnp.where(here_row < 2, head, panel[:block]))


    picked = lax.dynamic_index_in_dim(
        panel.reshape(col_blocks, ratio, block, 2, block), here_col // grid_rows, 1, keepdims=False
    )
    pairs = []
    for g in range(grid_rows):
        for s in range(grid_cols):
            dst_row = s % grid_rows
            dst_col = g + grid_rows * (s // grid_rows)
            pairs.append((g * grid_cols + s, dst_row * grid_cols + dst_col))
    across = lax.ppermute(picked, ("row", "col"), pairs)

    left = panel.reshape(height, 2 * block)
    right = across.reshape(width, 2 * block)
    update = jnp.dot(left, right.T, precision=lax.Precision.HIGH)
    result = base - jnp.where(full_i >= full_j, update, 0.0)
    panel_col = lax.dynamic_index_in_dim(panel, jnp.minimum(here_col, 1), 1, keepdims=False)
    result = result.at[:, :block].set(jnp.where(here_col < 2, panel_col, result[:, :block]))
    return result.reshape(row_blocks, 1, block, col_blocks, 1, block)


def solution(mesh):
    return jax.shard_map(
        shards,
        mesh=mesh,
        in_specs=(
            P(None, "row", None, None, "col", None),
            P(("row", "col"), None, None, None),
            P(("row", "col"), None, None),
            P(("row", "col"), None),
            P(("row", "col")),
            P(),
        ),
        out_specs=P(None, "row", None, None, "col", None),
        check_vma=False,
    )
```

```python
import jax
import jax.numpy as jnp
from jax import lax
from jax.sharding import PartitionSpec as P

HIGH = lax.Precision.HIGHEST


def symmetric(block):
    return jnp.tril(block) + jnp.swapaxes(jnp.tril(block, -1), -1, -2)


def lower_inverse(lower_factor):
    ident = jnp.eye(lower_factor.shape[0], dtype=lower_factor.dtype)
    return jax.scipy.linalg.solve_triangular(lower_factor, ident, lower=True)


def leading(block00, block10, block11, link):
    size = block00.shape[0]
    first = symmetric(block00)
    second = symmetric(block11)
    coupled = link * block10
    whole = jnp.concatenate(
        [jnp.concatenate([first, coupled.T], 1), jnp.concatenate([coupled, second], 1)], 0
    )
    ident = jnp.eye(2 * size, dtype=whole.dtype)
    spread = jnp.sum(jnp.abs(whole), axis=1) - jnp.abs(jnp.diagonal(whole))
    whole = whole * (1.0 - ident) + ident * (1.0 + spread)[:, None]
    factor00 = jnp.linalg.cholesky(whole[:size, :size])
    inv00 = lower_inverse(factor00)
    factor10 = jnp.dot(whole[size:, :size], inv00.T, precision=HIGH)
    reduced = whole[size:, size:] - jnp.dot(factor10, factor10.T, precision=HIGH)
    factor11 = jnp.linalg.cholesky(reduced)
    inv11 = lower_inverse(factor11)
    return factor00, factor10, factor11, inv00, inv11


def shards(hess, coupling, dest_row, local_row, live, pattern):
    grid_rows = lax.axis_size("row")
    grid_cols = lax.axis_size("col")
    here_row = lax.axis_index("row")
    here_col = lax.axis_index("col")
    row_blocks = hess.shape[0]
    col_blocks = hess.shape[3]
    block = hess.shape[2]
    slot_count = coupling.shape[1]
    bucket = slot_count // 4
    height = row_blocks * block
    width = col_blocks * block
    ratio = grid_cols // grid_rows
    mask = pattern.astype(jnp.float32)

    corner = hess[0, 0, :, 0, 0, :].astype(jnp.float32)
    devices = grid_rows * grid_cols
    here = here_row * grid_cols + here_col
    pivots = []
    for source in (0, grid_cols, grid_cols + 1):
        value = jnp.where(here == source, corner, 0.0)
        reach = 1
        while reach < devices:
            pairs = [
                ((source + m) % devices, (source + m + reach) % devices)
                for m in range(min(reach, devices - reach))
            ]
            value = value + lax.ppermute(value, ("row", "col"), pairs)
            reach *= 2
        pivots.append(value)

    grid_ids = jnp.arange(grid_rows, dtype=jnp.int32)
    dest = dest_row[0, :, 0]
    active = jnp.arange(slot_count, dtype=jnp.int32) < live[0]
    hits = (dest[:, None] == grid_ids[None, :]) & active[:, None]
    ranks = jnp.cumsum(hits.astype(jnp.int32), axis=0) - 1
    place = jnp.sum(jnp.where(hits, ranks + grid_ids[None, :] * bucket, 0), axis=1)
    place = jnp.where(active, place, -1)
    pick = jnp.arange(grid_rows * bucket, dtype=jnp.int32)[:, None] == place[None, :]
    outgoing = jnp.dot(
        pick.astype(jnp.float32), coupling[0].reshape(slot_count, 2 * block), precision=HIGH
    )
    labels = jnp.sum(jnp.where(pick, local_row[0][None, :], 0), axis=1).astype(jnp.float32)
    arrived = lax.all_to_all(
        outgoing.reshape(grid_rows, bucket, 2 * block), "row", split_axis=0, concat_axis=0, tiled=True
    )
    arrived_rows = lax.all_to_all(
        labels.reshape(grid_rows, bucket), "row", split_axis=0, concat_axis=0, tiled=True
    )
    spots = arrived_rows.reshape(-1).astype(jnp.int32)
    spread = jnp.arange(height, dtype=jnp.int32)[:, None] == spots[None, :]
    partial_value = jnp.dot(
        spread.astype(jnp.float32), arrived.reshape(-1, 2 * block), precision=HIGH
    ).reshape(height, 2, block)
    own = hess[:, 0, :, 0, 0, :].astype(jnp.float32).reshape(height, block)
    which = (jnp.arange(2, dtype=jnp.int32) == here_col).astype(jnp.float32)
    partial_value = partial_value + own[:, None, :] * which[None, :, None]

    mine = lax.dynamic_index_in_dim(
        mask.reshape(row_blocks, grid_rows, -1), here_row, 1, keepdims=False
    )
    rowmask = jnp.repeat(mine[:, :2], block, axis=0)
    partial_value, pivots = lax.optimization_barrier((partial_value, pivots))
    assembled = lax.psum(partial_value, "col") * rowmask[:, :, None]
    tiles = jnp.transpose(hess[:, 0, :, :, 0, :], (0, 2, 1, 3)).astype(jnp.float32)
    block_i = jnp.arange(row_blocks, dtype=jnp.int32) * grid_rows + here_row
    block_j = jnp.arange(col_blocks, dtype=jnp.int32) * grid_cols + here_col
    links = lax.dynamic_index_in_dim(
        lax.dynamic_index_in_dim(
            mask.reshape(row_blocks, grid_rows, col_blocks, grid_cols), here_row, 1, keepdims=False
        ),
        here_col,
        2,
        keepdims=False,
    )
    below = (block_i[:, None] > block_j[None, :])[:, :, None, None]
    kept = (block_i[:, None] >= block_j[None, :])[:, :, None, None]
    base = jnp.where(below, links[:, :, None, None] * tiles, 0.0)
    on_diag = here_row == here_col % grid_rows
    tri = jnp.arange(block)[:, None] >= jnp.arange(block)[None, :]
    for u in range(col_blocks):
        top = u * ratio + here_col // grid_rows
        own_tile = lax.dynamic_slice(tiles, (top, u, 0, 0), (1, 1, block, block))[0, 0]
        sym_tile = jnp.where(tri, own_tile, own_tile.T)
        old_tile = lax.dynamic_slice(base, (top, u, 0, 0), (1, 1, block, block))[0, 0]
        new_tile = jnp.where(on_diag, sym_tile, old_tile)
        base = lax.dynamic_update_slice(base, new_tile[None, None], (top, u, 0, 0))
    base, assembled = lax.optimization_barrier((base, assembled))
    f00, f10, f11, inv00, inv11 = leading(pivots[0], pivots[1], pivots[2], mask[1, 0])
    first = jnp.dot(assembled[:, 0], inv00.T, precision=HIGH)
    second = jnp.dot(
        assembled[:, 1] - jnp.dot(first, f10.T, precision=HIGH), inv11.T, precision=HIGH
    )
    panel = jnp.stack([first, second], 1)
    head_first = jnp.where(here_row == 0, f00, f10)
    head_second = jnp.where(here_row == 0, jnp.zeros_like(f11), f11)
    head = jnp.stack([head_first, head_second], 1)
    panel = panel.at[:block].set(jnp.where(here_row < 2, head, panel[:block]))


    picked = lax.dynamic_index_in_dim(
        panel.reshape(col_blocks, ratio, block, 2, block), here_col // grid_rows, 1, keepdims=False
    )
    pairs = []
    for g in range(grid_rows):
        for s in range(grid_cols):
            dst_row = s % grid_rows
            dst_col = g + grid_rows * (s // grid_rows)
            pairs.append((g * grid_cols + s, dst_row * grid_cols + dst_col))
    across = lax.ppermute(picked, ("row", "col"), pairs)

    left = panel.reshape(row_blocks, block, 2 * block)
    right = across.reshape(col_blocks, block, 2 * block)
    update = jnp.einsum("tak,ubk->tuab", left, right, precision=lax.Precision.HIGH)
    result = base - jnp.where(kept, update, 0.0)
    panel_col = lax.dynamic_index_in_dim(panel, jnp.minimum(here_col, 1), 1, keepdims=False)
    panel_col = panel_col.reshape(row_blocks, block, block)
    result = result.at[:, 0].set(jnp.where(here_col < 2, panel_col, result[:, 0]))
    result = jnp.transpose(result, (0, 2, 1, 3))
    return result.reshape(row_blocks, 1, block, col_blocks, 1, block)


def solution(mesh):
    return jax.shard_map(
        shards,
        mesh=mesh,
        in_specs=(
            P(None, "row", None, None, "col", None),
            P(("row", "col"), None, None, None),
            P(("row", "col"), None, None),
            P(("row", "col"), None),
            P(("row", "col")),
            P(),
        ),
        out_specs=P(None, "row", None, None, "col", None),
        check_vma=False,
    )
```

```python
import jax
import jax.numpy as jnp
from jax import lax
from jax.sharding import PartitionSpec as P

HIGH = lax.Precision.HIGHEST


def symmetric(block):
    return jnp.tril(block) + jnp.swapaxes(jnp.tril(block, -1), -1, -2)


def lower_inverse(lower_factor):
    ident = jnp.eye(lower_factor.shape[0], dtype=lower_factor.dtype)
    return jax.scipy.linalg.solve_triangular(lower_factor, ident, lower=True)


def leading(block00, block10, block11, link):
    size = block00.shape[0]
    first = symmetric(block00)
    second = symmetric(block11)
    coupled = link * block10
    whole = jnp.concatenate(
        [jnp.concatenate([first, coupled.T], 1), jnp.concatenate([coupled, second], 1)], 0
    )
    ident = jnp.eye(2 * size, dtype=whole.dtype)
    spread = jnp.sum(jnp.abs(whole), axis=1) - jnp.abs(jnp.diagonal(whole))
    whole = whole * (1.0 - ident) + ident * (1.0 + spread)[:, None]
    factor00 = jnp.linalg.cholesky(whole[:size, :size])
    inv00 = lower_inverse(factor00)
    factor10 = jnp.dot(whole[size:, :size], inv00.T, precision=HIGH)
    reduced = whole[size:, size:] - jnp.dot(factor10, factor10.T, precision=HIGH)
    factor11 = jnp.linalg.cholesky(reduced)
    inv11 = lower_inverse(factor11)
    return factor00, factor10, factor11, inv00, inv11


def shards(hess, coupling, dest_row, local_row, live, pattern):
    grid_rows = lax.axis_size("row")
    grid_cols = lax.axis_size("col")
    here_row = lax.axis_index("row")
    here_col = lax.axis_index("col")
    row_blocks = hess.shape[0]
    col_blocks = hess.shape[3]
    block = hess.shape[2]
    slot_count = coupling.shape[1]
    bucket = slot_count // 4
    height = row_blocks * block
    width = col_blocks * block
    ratio = grid_cols // grid_rows
    mask = pattern.astype(jnp.float32)

    corner = hess[0, 0, :, 0, 0, :].astype(jnp.float32)
    devices = grid_rows * grid_cols
    here = here_row * grid_cols + here_col
    pivots = []
    for source in (0, grid_cols, grid_cols + 1):
        value = jnp.where(here == source, corner, 0.0)
        reach = 1
        while reach < devices:
            pairs = [
                ((source + m) % devices, (source + m + reach) % devices)
                for m in range(min(reach, devices - reach))
            ]
            value = value + lax.ppermute(value, ("row", "col"), pairs)
            reach *= 2
        pivots.append(value)

    grid_ids = jnp.arange(grid_rows, dtype=jnp.int32)
    dest = dest_row[0, :, 0]
    active = jnp.arange(slot_count, dtype=jnp.int32) < live[0]
    hits = (dest[:, None] == grid_ids[None, :]) & active[:, None]
    ranks = jnp.cumsum(hits.astype(jnp.int32), axis=0) - 1
    place = jnp.sum(jnp.where(hits, ranks + grid_ids[None, :] * bucket, 0), axis=1)
    place = jnp.where(active, place, -1)
    pick = jnp.arange(grid_rows * bucket, dtype=jnp.int32)[:, None] == place[None, :]
    outgoing = jnp.dot(
        pick.astype(jnp.float32), coupling[0].reshape(slot_count, 2 * block), precision=HIGH
    )
    labels = jnp.sum(jnp.where(pick, local_row[0][None, :], 0), axis=1).astype(jnp.float32)
    arrived = lax.all_to_all(
        outgoing.reshape(grid_rows, bucket, 2 * block), "row", split_axis=0, concat_axis=0, tiled=True
    )
    arrived_rows = lax.all_to_all(
        labels.reshape(grid_rows, bucket), "row", split_axis=0, concat_axis=0, tiled=True
    )
    spots = arrived_rows.reshape(-1).astype(jnp.int32)
    spread = jnp.arange(height, dtype=jnp.int32)[:, None] == spots[None, :]
    partial_value = jnp.dot(
        spread.astype(jnp.float32), arrived.reshape(-1, 2 * block), precision=HIGH
    )
    own = hess[:, 0, :, 0, 0, :].astype(jnp.float32).reshape(height, block)
    which = (jnp.arange(2, dtype=jnp.int32) == here_col).astype(jnp.float32)
    which = jnp.repeat(which, block)
    partial_value = partial_value + jnp.concatenate([own, own], 1) * which[None, :]

    mine = lax.dynamic_index_in_dim(
        mask.reshape(row_blocks, grid_rows, -1), here_row, 1, keepdims=False
    )
    rowmask = jnp.repeat(jnp.repeat(mine[:, :2], block, axis=0), block, axis=1)
    assembled = lax.psum(partial_value, "col") * rowmask
    tiles = jnp.transpose(hess[:, 0, :, :, 0, :], (0, 2, 1, 3)).astype(jnp.float32)
    block_i = jnp.arange(row_blocks, dtype=jnp.int32) * grid_rows + here_row
    block_j = jnp.arange(col_blocks, dtype=jnp.int32) * grid_cols + here_col
    links = lax.dynamic_index_in_dim(
        lax.dynamic_index_in_dim(
            mask.reshape(row_blocks, grid_rows, col_blocks, grid_cols), here_row, 1, keepdims=False
        ),
        here_col,
        2,
        keepdims=False,
    )
    below = (block_i[:, None] > block_j[None, :])[:, :, None, None]
    kept = (block_i[:, None] >= block_j[None, :])[:, :, None, None]
    base = jnp.where(below, links[:, :, None, None] * tiles, 0.0)
    on_diag = here_row == here_col % grid_rows
    tri = jnp.arange(block)[:, None] >= jnp.arange(block)[None, :]
    for u in range(col_blocks):
        top = u * ratio + here_col // grid_rows
        own_tile = lax.dynamic_slice(tiles, (top, u, 0, 0), (1, 1, block, block))[0, 0]
        sym_tile = jnp.where(tri, own_tile, own_tile.T)
        old_tile = lax.dynamic_slice(base, (top, u, 0, 0), (1, 1, block, block))[0, 0]
        new_tile = jnp.where(on_diag, sym_tile, old_tile)
        base = lax.dynamic_update_slice(base, new_tile[None, None], (top, u, 0, 0))
    base = jnp.transpose(base, (0, 2, 1, 3)).reshape(height, width)
    base, assembled = lax.optimization_barrier((base, assembled))
    f00, f10, f11, inv00, inv11 = leading(pivots[0], pivots[1], pivots[2], mask[1, 0])
    first = jnp.dot(assembled[:, :block], inv00.T, precision=HIGH)
    second = jnp.dot(
        assembled[:, block:] - jnp.dot(first, f10.T, precision=HIGH), inv11.T, precision=HIGH
    )
    panel = jnp.concatenate([first, second], 1)
    head_first = jnp.where(here_row == 0, f00, f10)
    head_second = jnp.where(here_row == 0, jnp.zeros_like(f11), f11)
    head = jnp.concatenate([head_first, head_second], 1)
    panel = panel.at[:block].set(jnp.where(here_row < 2, head, panel[:block]))


    picked = lax.dynamic_index_in_dim(
        panel.reshape(col_blocks, ratio, block, 2 * block), here_col // grid_rows, 1, keepdims=False
    )
    pairs = []
    for g in range(grid_rows):
        for s in range(grid_cols):
            dst_row = s % grid_rows
            dst_col = g + grid_rows * (s // grid_rows)
            pairs.append((g * grid_cols + s, dst_row * grid_cols + dst_col))
    across = lax.ppermute(picked, ("row", "col"), pairs)

    right = across.reshape(width, 2 * block)
    update = jnp.dot(panel, right.T, precision=lax.Precision.HIGH)
    full_i = jnp.repeat(block_i, block)[:, None]
    full_j = jnp.repeat(block_j, block)[None, :]
    result = base - jnp.where(full_i >= full_j, update, 0.0)
    panel_col = lax.dynamic_slice_in_dim(panel, jnp.minimum(here_col, 1) * block, block, 1)
    result = result.at[:, :block].set(jnp.where(here_col < 2, panel_col, result[:, :block]))
    return result.reshape(row_blocks, 1, block, col_blocks, 1, block)


def solution(mesh):
    return jax.shard_map(
        shards,
        mesh=mesh,
        in_specs=(
            P(None, "row", None, None, "col", None),
            P(("row", "col"), None, None, None),
            P(("row", "col"), None, None),
            P(("row", "col"), None),
            P(("row", "col")),
            P(),
        ),
        out_specs=P(None, "row", None, None, "col", None),
        check_vma=False,
    )
```

```python
import jax
import jax.numpy as jnp
from jax import lax
from jax.sharding import PartitionSpec as P

HIGH = lax.Precision.HIGHEST


def symmetric(block):
    return jnp.tril(block) + jnp.swapaxes(jnp.tril(block, -1), -1, -2)


def lower_inverse(lower_factor):
    ident = jnp.eye(lower_factor.shape[0], dtype=lower_factor.dtype)
    return jax.scipy.linalg.solve_triangular(lower_factor, ident, lower=True)


def leading(block00, block10, block11, link):
    size = block00.shape[0]
    first = symmetric(block00)
    second = symmetric(block11)
    coupled = link * block10
    whole = jnp.concatenate(
        [jnp.concatenate([first, coupled.T], 1), jnp.concatenate([coupled, second], 1)], 0
    )
    ident = jnp.eye(2 * size, dtype=whole.dtype)
    spread = jnp.sum(jnp.abs(whole), axis=1) - jnp.abs(jnp.diagonal(whole))
    whole = whole * (1.0 - ident) + ident * (1.0 + spread)[:, None]
    factor00 = jnp.linalg.cholesky(whole[:size, :size])
    inv00 = lower_inverse(factor00)
    factor10 = jnp.dot(whole[size:, :size], inv00.T, precision=HIGH)
    reduced = whole[size:, size:] - jnp.dot(factor10, factor10.T, precision=HIGH)
    factor11 = jnp.linalg.cholesky(reduced)
    inv11 = lower_inverse(factor11)
    return factor00, factor10, factor11, inv00, inv11


def shards(hess, coupling, dest_row, local_row, live, pattern):
    grid_rows = lax.axis_size("row")
    grid_cols = lax.axis_size("col")
    here_row = lax.axis_index("row")
    here_col = lax.axis_index("col")
    row_blocks = hess.shape[0]
    col_blocks = hess.shape[3]
    block = hess.shape[2]
    slot_count = coupling.shape[1]
    bucket = slot_count // 4
    height = row_blocks * block
    width = col_blocks * block
    ratio = grid_cols // grid_rows
    mask = pattern.astype(jnp.float32)

    corner = hess[0, 0, :, 0, 0, :].astype(jnp.float32)
    devices = grid_rows * grid_cols
    here = here_row * grid_cols + here_col
    pivots = []
    for source in (0, grid_cols, grid_cols + 1):
        value = jnp.where(here == source, corner, 0.0)
        reach = 1
        while reach < devices:
            pairs = [
                ((source + m) % devices, (source + m + reach) % devices)
                for m in range(min(reach, devices - reach))
            ]
            value = value + lax.ppermute(value, ("row", "col"), pairs)
            reach *= 2
        pivots.append(value)

    grid_ids = jnp.arange(grid_rows, dtype=jnp.int32)
    dest = dest_row[0, :, 0]
    active = jnp.arange(slot_count, dtype=jnp.int32) < live[0]
    hits = (dest[:, None] == grid_ids[None, :]) & active[:, None]
    ranks = jnp.cumsum(hits.astype(jnp.int32), axis=0) - 1
    place = jnp.sum(jnp.where(hits, ranks + grid_ids[None, :] * bucket, 0), axis=1)
    place = jnp.where(active, place, -1)
    pick = jnp.arange(grid_rows * bucket, dtype=jnp.int32)[:, None] == place[None, :]
    outgoing = jnp.dot(
        pick.astype(jnp.float32), coupling[0].reshape(slot_count, 2 * block), precision=HIGH
    )
    labels = jnp.sum(jnp.where(pick, local_row[0][None, :], 0), axis=1).astype(jnp.float32)
    arrived = lax.all_to_all(
        outgoing.reshape(grid_rows, bucket, 2 * block), "row", split_axis=0, concat_axis=0, tiled=True
    )
    arrived_rows = lax.all_to_all(
        labels.reshape(grid_rows, bucket), "row", split_axis=0, concat_axis=0, tiled=True
    )
    spots = arrived_rows.reshape(-1).astype(jnp.int32)
    spread = jnp.arange(height, dtype=jnp.int32)[:, None] == spots[None, :]
    partial_value = jnp.dot(
        spread.astype(jnp.float32), arrived.reshape(-1, 2 * block), precision=HIGH
    )
    own = hess[:, 0, :, 0, 0, :].astype(jnp.float32).reshape(height, block)
    which = (jnp.arange(2, dtype=jnp.int32) == here_col).astype(jnp.float32)
    which = jnp.repeat(which, block)
    partial_value = partial_value + jnp.concatenate([own, own], 1) * which[None, :]

    mine = lax.dynamic_index_in_dim(
        mask.reshape(row_blocks, grid_rows, -1), here_row, 1, keepdims=False
    )
    rowmask = jnp.repeat(jnp.repeat(mine[:, :2], block, axis=0), block, axis=1)
    assembled = lax.psum(partial_value, "col") * rowmask
    f00, f10, f11, inv00, inv11 = leading(pivots[0], pivots[1], pivots[2], mask[1, 0])
    late_hess, inv11 = lax.optimization_barrier((hess, inv11))
    tiles = jnp.transpose(late_hess[:, 0, :, :, 0, :], (0, 2, 1, 3)).astype(jnp.float32)
    block_i = jnp.arange(row_blocks, dtype=jnp.int32) * grid_rows + here_row
    block_j = jnp.arange(col_blocks, dtype=jnp.int32) * grid_cols + here_col
    links = lax.dynamic_index_in_dim(
        lax.dynamic_index_in_dim(
            mask.reshape(row_blocks, grid_rows, col_blocks, grid_cols), here_row, 1, keepdims=False
        ),
        here_col,
        2,
        keepdims=False,
    )
    below = (block_i[:, None] > block_j[None, :])[:, :, None, None]
    base = jnp.where(below, links[:, :, None, None] * tiles, 0.0)
    on_diag = here_row == here_col % grid_rows
    tri = jnp.arange(block)[:, None] >= jnp.arange(block)[None, :]
    for u in range(col_blocks):
        top = u * ratio + here_col // grid_rows
        own_tile = lax.dynamic_slice(tiles, (top, u, 0, 0), (1, 1, block, block))[0, 0]
        sym_tile = jnp.where(tri, own_tile, own_tile.T)
        old_tile = lax.dynamic_slice(base, (top, u, 0, 0), (1, 1, block, block))[0, 0]
        new_tile = jnp.where(on_diag, sym_tile, old_tile)
        base = lax.dynamic_update_slice(base, new_tile[None, None], (top, u, 0, 0))
    base = jnp.transpose(base, (0, 2, 1, 3)).reshape(height, width)
    base, assembled = lax.optimization_barrier((base, assembled))
    first = jnp.dot(assembled[:, :block], inv00.T, precision=HIGH)
    second = jnp.dot(
        assembled[:, block:] - jnp.dot(first, f10.T, precision=HIGH), inv11.T, precision=HIGH
    )
    panel = jnp.concatenate([first, second], 1)
    head_first = jnp.where(here_row == 0, f00, f10)
    head_second = jnp.where(here_row == 0, jnp.zeros_like(f11), f11)
    head = jnp.concatenate([head_first, head_second], 1)
    panel = panel.at[:block].set(jnp.where(here_row < 2, head, panel[:block]))


    picked = lax.dynamic_index_in_dim(
        panel.reshape(col_blocks, ratio, block, 2 * block), here_col // grid_rows, 1, keepdims=False
    )
    pairs = []
    for g in range(grid_rows):
        for s in range(grid_cols):
            dst_row = s % grid_rows
            dst_col = g + grid_rows * (s // grid_rows)
            pairs.append((g * grid_cols + s, dst_row * grid_cols + dst_col))
    across = lax.ppermute(picked, ("row", "col"), pairs)

    right = across.reshape(width, 2 * block)
    update = jnp.dot(panel, right.T, precision=lax.Precision.HIGH)
    full_i = jnp.repeat(block_i, block)[:, None]
    full_j = jnp.repeat(block_j, block)[None, :]
    result = base - jnp.where(full_i >= full_j, update, 0.0)
    panel_col = lax.dynamic_slice_in_dim(panel, jnp.minimum(here_col, 1) * block, block, 1)
    result = result.at[:, :block].set(jnp.where(here_col < 2, panel_col, result[:, :block]))
    return result.reshape(row_blocks, 1, block, col_blocks, 1, block)


def solution(mesh):
    return jax.shard_map(
        shards,
        mesh=mesh,
        in_specs=(
            P(None, "row", None, None, "col", None),
            P(("row", "col"), None, None, None),
            P(("row", "col"), None, None),
            P(("row", "col"), None),
            P(("row", "col")),
            P(),
        ),
        out_specs=P(None, "row", None, None, "col", None),
        check_vma=False,
    )
```

```python
import jax
import jax.numpy as jnp
from jax import lax
from jax.sharding import PartitionSpec as P

HIGH = lax.Precision.HIGHEST


def symmetric(block):
    return jnp.tril(block) + jnp.swapaxes(jnp.tril(block, -1), -1, -2)


def lower_inverse(lower_factor):
    ident = jnp.eye(lower_factor.shape[0], dtype=lower_factor.dtype)
    return jax.scipy.linalg.solve_triangular(lower_factor, ident, lower=True)


def leading(block00, block10, block11, link):
    size = block00.shape[0]
    first = symmetric(block00)
    second = symmetric(block11)
    coupled = link * block10
    whole = jnp.concatenate(
        [jnp.concatenate([first, coupled.T], 1), jnp.concatenate([coupled, second], 1)], 0
    )
    ident = jnp.eye(2 * size, dtype=whole.dtype)
    spread = jnp.sum(jnp.abs(whole), axis=1) - jnp.abs(jnp.diagonal(whole))
    whole = whole * (1.0 - ident) + ident * (1.0 + spread)[:, None]
    factor00 = jnp.linalg.cholesky(whole[:size, :size])
    inv00 = lower_inverse(factor00)
    factor10 = jnp.dot(whole[size:, :size], inv00.T, precision=HIGH)
    reduced = whole[size:, size:] - jnp.dot(factor10, factor10.T, precision=HIGH)
    factor11 = jnp.linalg.cholesky(reduced)
    inv11 = lower_inverse(factor11)
    return factor00, factor10, factor11, inv00, inv11


def shards(hess, coupling, dest_row, local_row, live, pattern):
    grid_rows = lax.axis_size("row")
    grid_cols = lax.axis_size("col")
    here_row = lax.axis_index("row")
    here_col = lax.axis_index("col")
    row_blocks = hess.shape[0]
    col_blocks = hess.shape[3]
    block = hess.shape[2]
    slot_count = coupling.shape[1]
    bucket = slot_count // 4
    height = row_blocks * block
    width = col_blocks * block
    ratio = grid_cols // grid_rows
    mask = pattern.astype(jnp.float32)

    corner = hess[0, 0, :, 0, 0, :].astype(jnp.float32)
    devices = grid_rows * grid_cols
    here = here_row * grid_cols + here_col
    pivots = []
    for source in (0, grid_cols, grid_cols + 1):
        value = jnp.where(here == source, corner, 0.0)
        reach = 1
        while reach < devices:
            pairs = [
                ((source + m) % devices, (source + m + reach) % devices)
                for m in range(min(reach, devices - reach))
            ]
            value = value + lax.ppermute(value, ("row", "col"), pairs)
            reach *= 2
        pivots.append(value)

    grid_ids = jnp.arange(grid_rows, dtype=jnp.int32)
    dest = dest_row[0, :, 0]
    active = jnp.arange(slot_count, dtype=jnp.int32) < live[0]
    hits = (dest[:, None] == grid_ids[None, :]) & active[:, None]
    ranks = jnp.cumsum(hits.astype(jnp.int32), axis=0) - 1
    place = jnp.sum(jnp.where(hits, ranks + grid_ids[None, :] * bucket, 0), axis=1)
    place = jnp.where(active, place, -1)
    pick = jnp.arange(grid_rows * bucket, dtype=jnp.int32)[:, None] == place[None, :]
    outgoing = jnp.dot(
        pick.astype(jnp.float32), coupling[0].reshape(slot_count, 2 * block), precision=HIGH
    )
    labels = jnp.sum(jnp.where(pick, local_row[0][None, :], 0), axis=1).astype(jnp.float32)
    arrived = lax.all_to_all(
        outgoing.reshape(grid_rows, bucket, 2 * block), "row", split_axis=0, concat_axis=0, tiled=True
    )
    arrived_rows = lax.all_to_all(
        labels.reshape(grid_rows, bucket), "row", split_axis=0, concat_axis=0, tiled=True
    )
    spots = arrived_rows.reshape(-1).astype(jnp.int32)
    spread = jnp.arange(height, dtype=jnp.int32)[:, None] == spots[None, :]
    partial_value = jnp.dot(
        spread.astype(jnp.float32), arrived.reshape(-1, 2 * block), precision=HIGH
    )
    own = hess[:, 0, :, 0, 0, :].astype(jnp.float32).reshape(height, block)
    which = (jnp.arange(2, dtype=jnp.int32) == here_col).astype(jnp.float32)
    which = jnp.repeat(which, block)
    partial_value = partial_value + jnp.concatenate([own, own], 1) * which[None, :]

    mine = lax.dynamic_index_in_dim(
        mask.reshape(row_blocks, grid_rows, -1), here_row, 1, keepdims=False
    )
    rowmask = jnp.repeat(jnp.repeat(mine[:, :2], block, axis=0), block, axis=1)
    split = (row_blocks * 3 // 5) * block
    rest = height - split
    chunk = rest // grid_cols
    pieces = lax.all_to_all(
        partial_value[split:].reshape(grid_cols, chunk, 2 * block),
        "col",
        split_axis=0,
        concat_axis=0,
        tiled=True,
    )
    gathered = lax.all_to_all(
        jnp.broadcast_to(jnp.sum(pieces, axis=0)[None], (grid_cols, chunk, 2 * block)),
        "col",
        split_axis=0,
        concat_axis=0,
        tiled=True,
    ).reshape(rest, 2 * block)
    assembled = jnp.concatenate([lax.psum(partial_value[:split], "col"), gathered], 0) * rowmask
    f00, f10, f11, inv00, inv11 = leading(pivots[0], pivots[1], pivots[2], mask[1, 0])
    late_hess, inv11 = lax.optimization_barrier((hess, inv11))
    tiles = jnp.transpose(late_hess[:, 0, :, :, 0, :], (0, 2, 1, 3)).astype(jnp.float32)
    block_i = jnp.arange(row_blocks, dtype=jnp.int32) * grid_rows + here_row
    block_j = jnp.arange(col_blocks, dtype=jnp.int32) * grid_cols + here_col
    links = lax.dynamic_index_in_dim(
        lax.dynamic_index_in_dim(
            mask.reshape(row_blocks, grid_rows, col_blocks, grid_cols), here_row, 1, keepdims=False
        ),
        here_col,
        2,
        keepdims=False,
    )
    below = (block_i[:, None] > block_j[None, :])[:, :, None, None]
    base = jnp.where(below, links[:, :, None, None] * tiles, 0.0)
    on_diag = here_row == here_col % grid_rows
    tri = jnp.arange(block)[:, None] >= jnp.arange(block)[None, :]
    for u in range(col_blocks):
        top = u * ratio + here_col // grid_rows
        own_tile = lax.dynamic_slice(tiles, (top, u, 0, 0), (1, 1, block, block))[0, 0]
        sym_tile = jnp.where(tri, own_tile, own_tile.T)
        old_tile = lax.dynamic_slice(base, (top, u, 0, 0), (1, 1, block, block))[0, 0]
        new_tile = jnp.where(on_diag, sym_tile, old_tile)
        base = lax.dynamic_update_slice(base, new_tile[None, None], (top, u, 0, 0))
    base = jnp.transpose(base, (0, 2, 1, 3)).reshape(height, width)
    base, assembled = lax.optimization_barrier((base, assembled))
    first = jnp.dot(assembled[:, :block], inv00.T, precision=HIGH)
    second = jnp.dot(
        assembled[:, block:] - jnp.dot(first, f10.T, precision=HIGH), inv11.T, precision=HIGH
    )
    panel = jnp.concatenate([first, second], 1)
    head_first = jnp.where(here_row == 0, f00, f10)
    head_second = jnp.where(here_row == 0, jnp.zeros_like(f11), f11)
    head = jnp.concatenate([head_first, head_second], 1)
    panel = panel.at[:block].set(jnp.where(here_row < 2, head, panel[:block]))


    picked = lax.dynamic_index_in_dim(
        panel.reshape(col_blocks, ratio, block, 2 * block), here_col // grid_rows, 1, keepdims=False
    )
    pairs = []
    for g in range(grid_rows):
        for s in range(grid_cols):
            dst_row = s % grid_rows
            dst_col = g + grid_rows * (s // grid_rows)
            pairs.append((g * grid_cols + s, dst_row * grid_cols + dst_col))
    across = lax.ppermute(picked, ("row", "col"), pairs)

    right = across.reshape(width, 2 * block)
    update = jnp.dot(panel, right.T, precision=lax.Precision.HIGH)
    full_i = jnp.repeat(block_i, block)[:, None]
    full_j = jnp.repeat(block_j, block)[None, :]
    result = base - jnp.where(full_i >= full_j, update, 0.0)
    panel_col = lax.dynamic_slice_in_dim(panel, jnp.minimum(here_col, 1) * block, block, 1)
    result = result.at[:, :block].set(jnp.where(here_col < 2, panel_col, result[:, :block]))
    return result.reshape(row_blocks, 1, block, col_blocks, 1, block)


def solution(mesh):
    return jax.shard_map(
        shards,
        mesh=mesh,
        in_specs=(
            P(None, "row", None, None, "col", None),
            P(("row", "col"), None, None, None),
            P(("row", "col"), None, None),
            P(("row", "col"), None),
            P(("row", "col")),
            P(),
        ),
        out_specs=P(None, "row", None, None, "col", None),
        check_vma=False,
    )
```

```python
import jax
import jax.numpy as jnp
from jax import lax
from jax.sharding import PartitionSpec as P

HIGH = lax.Precision.HIGHEST


def symmetric(block):
    return jnp.tril(block) + jnp.swapaxes(jnp.tril(block, -1), -1, -2)


def lower_inverse(lower_factor):
    ident = jnp.eye(lower_factor.shape[0], dtype=lower_factor.dtype)
    return jax.scipy.linalg.solve_triangular(lower_factor, ident, lower=True)


def leading(block00, block10, block11, link):
    size = block00.shape[0]
    first = symmetric(block00)
    second = symmetric(block11)
    coupled = link * block10
    whole = jnp.concatenate(
        [jnp.concatenate([first, coupled.T], 1), jnp.concatenate([coupled, second], 1)], 0
    )
    ident = jnp.eye(2 * size, dtype=whole.dtype)
    spread = jnp.sum(jnp.abs(whole), axis=1) - jnp.abs(jnp.diagonal(whole))
    whole = whole * (1.0 - ident) + ident * (1.0 + spread)[:, None]
    factor00 = jnp.linalg.cholesky(whole[:size, :size])
    inv00 = lower_inverse(factor00)
    factor10 = jnp.dot(whole[size:, :size], inv00.T, precision=HIGH)
    reduced = whole[size:, size:] - jnp.dot(factor10, factor10.T, precision=HIGH)
    factor11 = jnp.linalg.cholesky(reduced)
    inv11 = lower_inverse(factor11)
    return factor00, factor10, factor11, inv00, inv11


def shards(hess, coupling, dest_row, local_row, live, pattern):
    grid_rows = lax.axis_size("row")
    grid_cols = lax.axis_size("col")
    here_row = lax.axis_index("row")
    here_col = lax.axis_index("col")
    row_blocks = hess.shape[0]
    col_blocks = hess.shape[3]
    block = hess.shape[2]
    slot_count = coupling.shape[1]
    bucket = slot_count // 4
    height = row_blocks * block
    width = col_blocks * block
    ratio = grid_cols // grid_rows
    mask = pattern.astype(jnp.float32)

    corner = hess[0, 0, :, 0, 0, :].astype(jnp.float32)
    devices = grid_rows * grid_cols
    here = here_row * grid_cols + here_col
    pivots = []
    for source in (0, grid_cols, grid_cols + 1):
        value = jnp.where(here == source, corner, 0.0)
        reach = 1
        while reach < devices:
            pairs = [
                ((source + m) % devices, (source + m + reach) % devices)
                for m in range(min(reach, devices - reach))
            ]
            value = value + lax.ppermute(value, ("row", "col"), pairs)
            reach *= 2
        pivots.append(value)

    grid_ids = jnp.arange(grid_rows, dtype=jnp.int32)
    dest = dest_row[0, :, 0]
    active = jnp.arange(slot_count, dtype=jnp.int32) < live[0]
    hits = (dest[:, None] == grid_ids[None, :]) & active[:, None]
    ranks = jnp.cumsum(hits.astype(jnp.int32), axis=0) - 1
    place = jnp.sum(jnp.where(hits, ranks + grid_ids[None, :] * bucket, 0), axis=1)
    place = jnp.where(active, place, -1)
    pick = jnp.arange(grid_rows * bucket, dtype=jnp.int32)[:, None] == place[None, :]
    outgoing = jnp.dot(
        pick.astype(jnp.float32), coupling[0].reshape(slot_count, 2 * block), precision=HIGH
    )
    labels = jnp.sum(jnp.where(pick, local_row[0][None, :], 0), axis=1).astype(jnp.float32)
    arrived = lax.all_to_all(
        outgoing.reshape(grid_rows, bucket, 2 * block), "row", split_axis=0, concat_axis=0, tiled=True
    )
    arrived_rows = lax.all_to_all(
        labels.reshape(grid_rows, bucket), "row", split_axis=0, concat_axis=0, tiled=True
    )
    spots = arrived_rows.reshape(-1).astype(jnp.int32)
    spread = jnp.arange(height, dtype=jnp.int32)[:, None] == spots[None, :]
    partial_value = jnp.dot(
        spread.astype(jnp.float32), arrived.reshape(-1, 2 * block), precision=HIGH
    )
    own = hess[:, 0, :, 0, 0, :].astype(jnp.float32).reshape(height, block)
    which = (jnp.arange(2, dtype=jnp.int32) == here_col).astype(jnp.float32)
    which = jnp.repeat(which, block)
    partial_value = partial_value + jnp.concatenate([own, own], 1) * which[None, :]

    mine = lax.dynamic_index_in_dim(
        mask.reshape(row_blocks, grid_rows, -1), here_row, 1, keepdims=False
    )
    rowmask = jnp.repeat(jnp.repeat(mine[:, :2], block, axis=0), block, axis=1)
    assembled = lax.psum(partial_value, "col") * rowmask
    f00, f10, f11, inv00, inv11 = leading(pivots[0], pivots[1], pivots[2], mask[1, 0])
    late_hess, inv11 = lax.optimization_barrier((hess, inv11))
    tiles = jnp.transpose(late_hess[:, 0, :, :, 0, :], (0, 2, 1, 3)).astype(jnp.float32)
    block_i = jnp.arange(row_blocks, dtype=jnp.int32) * grid_rows + here_row
    block_j = jnp.arange(col_blocks, dtype=jnp.int32) * grid_cols + here_col
    links = lax.dynamic_index_in_dim(
        lax.dynamic_index_in_dim(
            mask.reshape(row_blocks, grid_rows, col_blocks, grid_cols), here_row, 1, keepdims=False
        ),
        here_col,
        2,
        keepdims=False,
    )
    below = (block_i[:, None] > block_j[None, :])[:, :, None, None]
    base = jnp.where(below, links[:, :, None, None] * tiles, 0.0)
    on_diag = here_row == here_col % grid_rows
    tri = jnp.arange(block)[:, None] >= jnp.arange(block)[None, :]
    for u in range(col_blocks):
        top = u * ratio + here_col // grid_rows
        own_tile = lax.dynamic_slice(tiles, (top, u, 0, 0), (1, 1, block, block))[0, 0]
        sym_tile = jnp.where(tri, own_tile, own_tile.T)
        old_tile = lax.dynamic_slice(base, (top, u, 0, 0), (1, 1, block, block))[0, 0]
        new_tile = jnp.where(on_diag, sym_tile, old_tile)
        base = lax.dynamic_update_slice(base, new_tile[None, None], (top, u, 0, 0))
    base = jnp.transpose(base, (0, 2, 1, 3)).reshape(height, width)
    base, assembled = lax.optimization_barrier((base, assembled))
    def solve(rows):
        first = jnp.dot(rows[:, :block], inv00.T, precision=HIGH)
        second = jnp.dot(
            rows[:, block:] - jnp.dot(first, f10.T, precision=HIGH), inv11.T, precision=HIGH
        )
        return jnp.concatenate([first, second], 1)

    head_first = jnp.where(here_row == 0, f00, f10)
    head_second = jnp.where(here_row == 0, jnp.zeros_like(f11), f11)
    head = jnp.concatenate([head_first, head_second], 1)
    offset = here_col // grid_rows
    chosen = lax.dynamic_index_in_dim(
        assembled.reshape(col_blocks, ratio, block, 2 * block), offset, 1, keepdims=False
    )
    picked = solve(chosen.reshape(width, 2 * block)).reshape(col_blocks, block, 2 * block)
    picked = picked.at[0].set(jnp.where((here_row < 2) & (offset == 0), head, picked[0]))
    pairs = []
    for g in range(grid_rows):
        for s in range(grid_cols):
            dst_row = s % grid_rows
            dst_col = g + grid_rows * (s // grid_rows)
            pairs.append((g * grid_cols + s, dst_row * grid_cols + dst_col))
    across = lax.ppermute(picked, ("row", "col"), pairs)

    panel = solve(assembled)
    panel = panel.at[:block].set(jnp.where(here_row < 2, head, panel[:block]))

    right = across.reshape(width, 2 * block)
    update = jnp.dot(panel, right.T, precision=lax.Precision.HIGH)
    full_i = jnp.repeat(block_i, block)[:, None]
    full_j = jnp.repeat(block_j, block)[None, :]
    result = base - jnp.where(full_i >= full_j, update, 0.0)
    panel_col = lax.dynamic_slice_in_dim(panel, jnp.minimum(here_col, 1) * block, block, 1)
    result = result.at[:, :block].set(jnp.where(here_col < 2, panel_col, result[:, :block]))
    return result.reshape(row_blocks, 1, block, col_blocks, 1, block)


def solution(mesh):
    return jax.shard_map(
        shards,
        mesh=mesh,
        in_specs=(
            P(None, "row", None, None, "col", None),
            P(("row", "col"), None, None, None),
            P(("row", "col"), None, None),
            P(("row", "col"), None),
            P(("row", "col")),
            P(),
        ),
        out_specs=P(None, "row", None, None, "col", None),
        check_vma=False,
    )
```

```python
import jax
import jax.numpy as jnp
from jax import lax
from jax.sharding import PartitionSpec as P

HIGH = lax.Precision.HIGHEST


def symmetric(block):
    return jnp.tril(block) + jnp.swapaxes(jnp.tril(block, -1), -1, -2)


def lower_inverse(lower_factor):
    ident = jnp.eye(lower_factor.shape[0], dtype=lower_factor.dtype)
    return jax.scipy.linalg.solve_triangular(lower_factor, ident, lower=True)


def leading(block00, block10, block11, link):
    size = block00.shape[0]
    first = symmetric(block00)
    second = symmetric(block11)
    coupled = link * block10
    whole = jnp.concatenate(
        [jnp.concatenate([first, coupled.T], 1), jnp.concatenate([coupled, second], 1)], 0
    )
    ident = jnp.eye(2 * size, dtype=whole.dtype)
    spread = jnp.sum(jnp.abs(whole), axis=1) - jnp.abs(jnp.diagonal(whole))
    whole = whole * (1.0 - ident) + ident * (1.0 + spread)[:, None]
    factor00 = jnp.linalg.cholesky(whole[:size, :size])
    inv00 = lower_inverse(factor00)
    factor10 = jnp.dot(whole[size:, :size], inv00.T, precision=HIGH)
    reduced = whole[size:, size:] - jnp.dot(factor10, factor10.T, precision=HIGH)
    factor11 = jnp.linalg.cholesky(reduced)
    inv11 = lower_inverse(factor11)
    return factor00, factor10, factor11, inv00, inv11


def shards(hess, coupling, dest_row, local_row, live, pattern):
    grid_rows = lax.axis_size("row")
    grid_cols = lax.axis_size("col")
    here_row = lax.axis_index("row")
    here_col = lax.axis_index("col")
    row_blocks = hess.shape[0]
    col_blocks = hess.shape[3]
    block = hess.shape[2]
    slot_count = coupling.shape[1]
    bucket = slot_count // 4
    height = row_blocks * block
    width = col_blocks * block
    ratio = grid_cols // grid_rows
    mask = pattern.astype(jnp.float32)

    corner = hess[0, 0, :, 0, 0, :].astype(jnp.float32)
    devices = grid_rows * grid_cols
    here = here_row * grid_cols + here_col
    pivots = []
    for source in (0, grid_cols, grid_cols + 1):
        value = jnp.where(here == source, corner, 0.0)
        reach = 1
        while reach < devices:
            pairs = [
                ((source + m) % devices, (source + m + reach) % devices)
                for m in range(min(reach, devices - reach))
            ]
            value = value + lax.ppermute(value, ("row", "col"), pairs)
            reach *= 2
        pivots.append(value)

    grid_ids = jnp.arange(grid_rows, dtype=jnp.int32)
    dest = dest_row[0, :, 0]
    active = jnp.arange(slot_count, dtype=jnp.int32) < live[0]
    hits = (dest[:, None] == grid_ids[None, :]) & active[:, None]
    ranks = jnp.cumsum(hits.astype(jnp.int32), axis=0) - 1
    place = jnp.sum(jnp.where(hits, ranks + grid_ids[None, :] * bucket, 0), axis=1)
    place = jnp.where(active, place, -1)
    pick = jnp.arange(grid_rows * bucket, dtype=jnp.int32)[:, None] == place[None, :]
    outgoing = jnp.dot(
        pick.astype(jnp.float32), coupling[0].reshape(slot_count, 2 * block), precision=HIGH
    )
    labels = jnp.sum(jnp.where(pick, local_row[0][None, :], 0), axis=1).astype(jnp.float32)
    arrived = lax.all_to_all(
        outgoing.reshape(grid_rows, bucket, 2 * block), "row", split_axis=0, concat_axis=0, tiled=True
    )
    arrived_rows = lax.all_to_all(
        labels.reshape(grid_rows, bucket), "row", split_axis=0, concat_axis=0, tiled=True
    )
    spots = arrived_rows.reshape(-1).astype(jnp.int32)
    spread = jnp.arange(height, dtype=jnp.int32)[:, None] == spots[None, :]
    partial_value = jnp.dot(
        spread.astype(jnp.float32), arrived.reshape(-1, 2 * block), precision=HIGH
    )
    own = hess[:, 0, :, 0, 0, :].astype(jnp.float32).reshape(height, block)
    which = (jnp.arange(2, dtype=jnp.int32) == here_col).astype(jnp.float32)
    which = jnp.repeat(which, block)
    partial_value = partial_value + jnp.concatenate([own, own], 1) * which[None, :]

    mine = lax.dynamic_index_in_dim(
        mask.reshape(row_blocks, grid_rows, -1), here_row, 1, keepdims=False
    )
    rowmask = jnp.repeat(jnp.repeat(mine[:, :2], block, axis=0), block, axis=1)
    assembled = lax.psum(partial_value, "col") * rowmask
    f00, f10, f11, inv00, inv11 = leading(pivots[0], pivots[1], pivots[2], mask[1, 0])
    late_hess, inv11 = lax.optimization_barrier((hess, inv11))
    tiles = jnp.transpose(late_hess[:, 0, :, :, 0, :], (0, 2, 1, 3)).astype(jnp.float32)
    block_i = jnp.arange(row_blocks, dtype=jnp.int32) * grid_rows + here_row
    block_j = jnp.arange(col_blocks, dtype=jnp.int32) * grid_cols + here_col
    links = lax.dynamic_index_in_dim(
        lax.dynamic_index_in_dim(
            mask.reshape(row_blocks, grid_rows, col_blocks, grid_cols), here_row, 1, keepdims=False
        ),
        here_col,
        2,
        keepdims=False,
    )
    below = (block_i[:, None] > block_j[None, :])[:, :, None, None]
    base = jnp.where(below, links[:, :, None, None] * tiles, 0.0)
    on_diag = here_row == here_col % grid_rows
    tri = jnp.arange(block)[:, None] >= jnp.arange(block)[None, :]
    for u in range(col_blocks):
        top = u * ratio + here_col // grid_rows
        own_tile = lax.dynamic_slice(tiles, (top, u, 0, 0), (1, 1, block, block))[0, 0]
        sym_tile = jnp.where(tri, own_tile, own_tile.T)
        old_tile = lax.dynamic_slice(base, (top, u, 0, 0), (1, 1, block, block))[0, 0]
        new_tile = jnp.where(on_diag, sym_tile, old_tile)
        base = lax.dynamic_update_slice(base, new_tile[None, None], (top, u, 0, 0))
    base = jnp.transpose(base, (0, 2, 1, 3)).reshape(height, width)
    base, assembled = lax.optimization_barrier((base, assembled))
    def solve(rows):
        first = jnp.dot(rows[:, :block], inv00.T, precision=HIGH)
        second = jnp.dot(
            rows[:, block:] - jnp.dot(first, f10.T, precision=HIGH), inv11.T, precision=HIGH
        )
        return jnp.concatenate([first, second], 1)

    head_first = jnp.where(here_row == 0, f00, f10)
    head_second = jnp.where(here_row == 0, jnp.zeros_like(f11), f11)
    head = jnp.concatenate([head_first, head_second], 1)
    offset = here_col // grid_rows
    chosen = lax.dynamic_index_in_dim(
        assembled.reshape(col_blocks, ratio, block, 2 * block), offset, 1, keepdims=False
    )
    picked = solve(chosen.reshape(width, 2 * block)).reshape(col_blocks, block, 2 * block)
    picked = picked.at[0].set(jnp.where((here_row < 2) & (offset == 0), head, picked[0]))
    pairs = []
    for g in range(grid_rows):
        for s in range(grid_cols):
            dst_row = s % grid_rows
            dst_col = g + grid_rows * (s // grid_rows)
            pairs.append((g * grid_cols + s, dst_row * grid_cols + dst_col))
    across = lax.ppermute(picked, ("row", "col"), pairs)

    panel = solve(assembled)
    panel = panel.at[:block].set(jnp.where(here_row < 2, head, panel[:block]))

    right = across.reshape(width, 2 * block)
    update = jnp.dot(panel, right.T, precision=lax.Precision.HIGH)
    full_i = jnp.repeat(block_i, block)[:, None]
    full_j = jnp.repeat(block_j, block)[None, :]
    panel_col = lax.dynamic_slice_in_dim(panel, jnp.minimum(here_col, 1) * block, block, 1)
    spread_col = jnp.broadcast_to(panel_col[:, None, :], (height, col_blocks, block))
    in_panel = (full_j < 2) & (full_j == here_col)
    result = jnp.where(
        in_panel,
        spread_col.reshape(height, width),
        base - jnp.where(full_i >= full_j, update, 0.0),
    )
    return result.reshape(row_blocks, 1, block, col_blocks, 1, block)


def solution(mesh):
    return jax.shard_map(
        shards,
        mesh=mesh,
        in_specs=(
            P(None, "row", None, None, "col", None),
            P(("row", "col"), None, None, None),
            P(("row", "col"), None, None),
            P(("row", "col"), None),
            P(("row", "col")),
            P(),
        ),
        out_specs=P(None, "row", None, None, "col", None),
        check_vma=False,
    )
```

```python
import jax
import jax.numpy as jnp
from jax import lax
from jax.sharding import PartitionSpec as P

HIGH = lax.Precision.HIGHEST


def symmetric(block):
    return jnp.tril(block) + jnp.swapaxes(jnp.tril(block, -1), -1, -2)


def lower_inverse(lower_factor):
    ident = jnp.eye(lower_factor.shape[0], dtype=lower_factor.dtype)
    return jax.scipy.linalg.solve_triangular(lower_factor, ident, lower=True)


def leading(block00, block10, block11, link):
    size = block00.shape[0]
    first = symmetric(block00)
    second = symmetric(block11)
    coupled = link * block10
    whole = jnp.concatenate(
        [jnp.concatenate([first, coupled.T], 1), jnp.concatenate([coupled, second], 1)], 0
    )
    ident = jnp.eye(2 * size, dtype=whole.dtype)
    spread = jnp.sum(jnp.abs(whole), axis=1) - jnp.abs(jnp.diagonal(whole))
    whole = whole * (1.0 - ident) + ident * (1.0 + spread)[:, None]
    factor00 = jnp.linalg.cholesky(whole[:size, :size])
    inv00 = lower_inverse(factor00)
    factor10 = jnp.dot(whole[size:, :size], inv00.T, precision=HIGH)
    reduced = whole[size:, size:] - jnp.dot(factor10, factor10.T, precision=HIGH)
    factor11 = jnp.linalg.cholesky(reduced)
    inv11 = lower_inverse(factor11)
    return factor00, factor10, factor11, inv00, inv11


def shards(hess, coupling, dest_row, local_row, live, pattern):
    grid_rows = lax.axis_size("row")
    grid_cols = lax.axis_size("col")
    here_row = lax.axis_index("row")
    here_col = lax.axis_index("col")
    row_blocks = hess.shape[0]
    col_blocks = hess.shape[3]
    block = hess.shape[2]
    slot_count = coupling.shape[1]
    bucket = slot_count // 4
    height = row_blocks * block
    width = col_blocks * block
    ratio = grid_cols // grid_rows
    mask = pattern.astype(jnp.float32)

    corner = hess[0, 0, :, 0, 0, :].astype(jnp.float32)
    devices = grid_rows * grid_cols
    here = here_row * grid_cols + here_col
    pivots = []
    for source in (0, grid_cols, grid_cols + 1):
        value = jnp.where(here == source, corner, 0.0)
        reach = 1
        while reach < devices:
            pairs = [
                ((source + m) % devices, (source + m + reach) % devices)
                for m in range(min(reach, devices - reach))
            ]
            value = value + lax.ppermute(value, ("row", "col"), pairs)
            reach *= 2
        pivots.append(value)

    grid_ids = jnp.arange(grid_rows, dtype=jnp.int32)
    dest = dest_row[0, :, 0]
    active = jnp.arange(slot_count, dtype=jnp.int32) < live[0]
    hits = (dest[:, None] == grid_ids[None, :]) & active[:, None]
    ranks = jnp.cumsum(hits.astype(jnp.int32), axis=0) - 1
    place = jnp.sum(jnp.where(hits, ranks + grid_ids[None, :] * bucket, 0), axis=1)
    place = jnp.where(active, place, -1)
    pick = jnp.arange(grid_rows * bucket, dtype=jnp.int32)[:, None] == place[None, :]
    outgoing = jnp.dot(
        pick.astype(jnp.float32), coupling[0].reshape(slot_count, 2 * block), precision=HIGH
    )
    labels = jnp.sum(jnp.where(pick, local_row[0][None, :], 0), axis=1).astype(jnp.float32)
    arrived = lax.all_to_all(
        outgoing.reshape(grid_rows, bucket, 2 * block), "row", split_axis=0, concat_axis=0, tiled=True
    )
    arrived_rows = lax.all_to_all(
        labels.reshape(grid_rows, bucket), "row", split_axis=0, concat_axis=0, tiled=True
    )
    spots = arrived_rows.reshape(-1).astype(jnp.int32)
    spread = jnp.arange(height, dtype=jnp.int32)[:, None] == spots[None, :]
    partial_value = jnp.dot(
        spread.astype(jnp.float32), arrived.reshape(-1, 2 * block), precision=HIGH
    )
    own = hess[:, 0, :, 0, 0, :].astype(jnp.float32).reshape(height, block)
    which = (jnp.arange(2, dtype=jnp.int32) == here_col).astype(jnp.float32)
    which = jnp.repeat(which, block)
    partial_value = partial_value + jnp.concatenate([own, own], 1) * which[None, :]

    mine = lax.dynamic_index_in_dim(
        mask.reshape(row_blocks, grid_rows, -1), here_row, 1, keepdims=False
    )
    rowmask = jnp.repeat(jnp.repeat(mine[:, :2], block, axis=0), block, axis=1)
    assembled = lax.psum(partial_value * rowmask, "col")
    f00, f10, f11, inv00, inv11 = leading(pivots[0], pivots[1], pivots[2], mask[1, 0])
    late_hess, inv11 = lax.optimization_barrier((hess, inv11))
    tiles = jnp.transpose(late_hess[:, 0, :, :, 0, :], (0, 2, 1, 3)).astype(jnp.float32)
    block_i = jnp.arange(row_blocks, dtype=jnp.int32) * grid_rows + here_row
    block_j = jnp.arange(col_blocks, dtype=jnp.int32) * grid_cols + here_col
    links = lax.dynamic_index_in_dim(
        lax.dynamic_index_in_dim(
            mask.reshape(row_blocks, grid_rows, col_blocks, grid_cols), here_row, 1, keepdims=False
        ),
        here_col,
        2,
        keepdims=False,
    )
    below = (block_i[:, None] > block_j[None, :])[:, :, None, None]
    base = jnp.where(below, links[:, :, None, None] * tiles, 0.0)
    on_diag = here_row == here_col % grid_rows
    tri = jnp.arange(block)[:, None] >= jnp.arange(block)[None, :]
    for u in range(col_blocks):
        top = u * ratio + here_col // grid_rows
        own_tile = lax.dynamic_slice(tiles, (top, u, 0, 0), (1, 1, block, block))[0, 0]
        sym_tile = jnp.where(tri, own_tile, own_tile.T)
        old_tile = lax.dynamic_slice(base, (top, u, 0, 0), (1, 1, block, block))[0, 0]
        new_tile = jnp.where(on_diag, sym_tile, old_tile)
        base = lax.dynamic_update_slice(base, new_tile[None, None], (top, u, 0, 0))
    base = jnp.transpose(base, (0, 2, 1, 3)).reshape(height, width)
    base, assembled = lax.optimization_barrier((base, assembled))
    def solve(rows):
        first = jnp.dot(rows[:, :block], inv00.T, precision=HIGH)
        second = jnp.dot(
            rows[:, block:] - jnp.dot(first, f10.T, precision=HIGH), inv11.T, precision=HIGH
        )
        return jnp.concatenate([first, second], 1)

    head_first = jnp.where(here_row == 0, f00, f10)
    head_second = jnp.where(here_row == 0, jnp.zeros_like(f11), f11)
    head = jnp.concatenate([head_first, head_second], 1)
    offset = here_col // grid_rows
    chosen = lax.dynamic_index_in_dim(
        assembled.reshape(col_blocks, ratio, block, 2 * block), offset, 1, keepdims=False
    )
    picked = solve(chosen.reshape(width, 2 * block)).reshape(col_blocks, block, 2 * block)
    picked = picked.at[0].set(jnp.where((here_row < 2) & (offset == 0), head, picked[0]))
    pairs = []
    for g in range(grid_rows):
        for s in range(grid_cols):
            dst_row = s % grid_rows
            dst_col = g + grid_rows * (s // grid_rows)
            pairs.append((g * grid_cols + s, dst_row * grid_cols + dst_col))
    across = lax.ppermute(picked, ("row", "col"), pairs)

    panel = solve(assembled)
    panel = panel.at[:block].set(jnp.where(here_row < 2, head, panel[:block]))

    right = across.reshape(width, 2 * block)
    update = jnp.dot(panel, right.T, precision=lax.Precision.HIGH)
    full_i = jnp.repeat(block_i, block)[:, None]
    full_j = jnp.repeat(block_j, block)[None, :]
    result = base - jnp.where(full_i >= full_j, update, 0.0)
    panel_col = lax.dynamic_slice_in_dim(panel, jnp.minimum(here_col, 1) * block, block, 1)
    result = result.at[:, :block].set(jnp.where(here_col < 2, panel_col, result[:, :block]))
    return result.reshape(row_blocks, 1, block, col_blocks, 1, block)


def solution(mesh):
    return jax.shard_map(
        shards,
        mesh=mesh,
        in_specs=(
            P(None, "row", None, None, "col", None),
            P(("row", "col"), None, None, None),
            P(("row", "col"), None, None),
            P(("row", "col"), None),
            P(("row", "col")),
            P(),
        ),
        out_specs=P(None, "row", None, None, "col", None),
        check_vma=False,
    )
```

```python
import jax
import jax.numpy as jnp
from jax import lax
from jax.sharding import PartitionSpec as P

HIGH = lax.Precision.HIGHEST


def symmetric(block):
    return jnp.tril(block) + jnp.swapaxes(jnp.tril(block, -1), -1, -2)


def lower_inverse(lower_factor):
    ident = jnp.eye(lower_factor.shape[0], dtype=lower_factor.dtype)
    return jax.scipy.linalg.solve_triangular(lower_factor, ident, lower=True)


def leading(block00, block10, block11, link):
    size = block00.shape[0]
    first = symmetric(block00)
    second = symmetric(block11)
    coupled = link * block10
    whole = jnp.concatenate(
        [jnp.concatenate([first, coupled.T], 1), jnp.concatenate([coupled, second], 1)], 0
    )
    ident = jnp.eye(2 * size, dtype=whole.dtype)
    spread = jnp.sum(jnp.abs(whole), axis=1) - jnp.abs(jnp.diagonal(whole))
    whole = whole * (1.0 - ident) + ident * (1.0 + spread)[:, None]
    factor00 = jnp.linalg.cholesky(whole[:size, :size])
    inv00 = lower_inverse(factor00)
    factor10 = jnp.dot(whole[size:, :size], inv00.T, precision=HIGH)
    reduced = whole[size:, size:] - jnp.dot(factor10, factor10.T, precision=HIGH)
    factor11 = jnp.linalg.cholesky(reduced)
    inv11 = lower_inverse(factor11)
    return factor00, factor10, factor11, inv00, inv11


def shards(hess, coupling, dest_row, local_row, live, pattern):
    grid_rows = lax.axis_size("row")
    grid_cols = lax.axis_size("col")
    here_row = lax.axis_index("row")
    here_col = lax.axis_index("col")
    row_blocks = hess.shape[0]
    col_blocks = hess.shape[3]
    block = hess.shape[2]
    slot_count = coupling.shape[1]
    bucket = slot_count // 4
    height = row_blocks * block
    width = col_blocks * block
    ratio = grid_cols // grid_rows
    mask = pattern.astype(jnp.float32)

    corner = hess[0, 0, :, 0, 0, :].astype(jnp.float32)
    devices = grid_rows * grid_cols
    here = here_row * grid_cols + here_col
    gathered = [jnp.where(here == 0, corner, 0.0)]
    for source in (grid_cols, grid_cols + 1):
        gathered.append(lax.ppermute(jnp.where(here == source, corner, 0.0), ("row", "col"), [(source, 0)]))
    value = jnp.stack(gathered)
    reach = 1
    while reach < devices:
        pairs = [(m, m + reach) for m in range(min(reach, devices - reach))]
        value = value + lax.ppermute(value, ("row", "col"), pairs)
        reach *= 2
    pivots = [value[0], value[1], value[2]]

    grid_ids = jnp.arange(grid_rows, dtype=jnp.int32)
    dest = dest_row[0, :, 0]
    active = jnp.arange(slot_count, dtype=jnp.int32) < live[0]
    hits = (dest[:, None] == grid_ids[None, :]) & active[:, None]
    ranks = jnp.cumsum(hits.astype(jnp.int32), axis=0) - 1
    place = jnp.sum(jnp.where(hits, ranks + grid_ids[None, :] * bucket, 0), axis=1)
    place = jnp.where(active, place, -1)
    pick = jnp.arange(grid_rows * bucket, dtype=jnp.int32)[:, None] == place[None, :]
    outgoing = jnp.dot(
        pick.astype(jnp.float32), coupling[0].reshape(slot_count, 2 * block), precision=HIGH
    )
    labels = jnp.sum(jnp.where(pick, local_row[0][None, :], 0), axis=1).astype(jnp.float32)
    arrived = lax.all_to_all(
        outgoing.reshape(grid_rows, bucket, 2 * block), "row", split_axis=0, concat_axis=0, tiled=True
    )
    arrived_rows = lax.all_to_all(
        labels.reshape(grid_rows, bucket), "row", split_axis=0, concat_axis=0, tiled=True
    )
    spots = arrived_rows.reshape(-1).astype(jnp.int32)
    spread = jnp.arange(height, dtype=jnp.int32)[:, None] == spots[None, :]
    partial_value = jnp.dot(
        spread.astype(jnp.float32), arrived.reshape(-1, 2 * block), precision=HIGH
    )
    own = hess[:, 0, :, 0, 0, :].astype(jnp.float32).reshape(height, block)
    which = (jnp.arange(2, dtype=jnp.int32) == here_col).astype(jnp.float32)
    which = jnp.repeat(which, block)
    partial_value = partial_value + jnp.concatenate([own, own], 1) * which[None, :]

    mine = lax.dynamic_index_in_dim(
        mask.reshape(row_blocks, grid_rows, -1), here_row, 1, keepdims=False
    )
    rowmask = jnp.repeat(jnp.repeat(mine[:, :2], block, axis=0), block, axis=1)
    assembled = lax.psum(partial_value * rowmask, "col")
    f00, f10, f11, inv00, inv11 = leading(pivots[0], pivots[1], pivots[2], mask[1, 0])
    late_hess, inv11 = lax.optimization_barrier((hess, inv11))
    tiles = jnp.transpose(late_hess[:, 0, :, :, 0, :], (0, 2, 1, 3)).astype(jnp.float32)
    block_i = jnp.arange(row_blocks, dtype=jnp.int32) * grid_rows + here_row
    block_j = jnp.arange(col_blocks, dtype=jnp.int32) * grid_cols + here_col
    links = lax.dynamic_index_in_dim(
        lax.dynamic_index_in_dim(
            mask.reshape(row_blocks, grid_rows, col_blocks, grid_cols), here_row, 1, keepdims=False
        ),
        here_col,
        2,
        keepdims=False,
    )
    below = (block_i[:, None] > block_j[None, :])[:, :, None, None]
    base = jnp.where(below, links[:, :, None, None] * tiles, 0.0)
    on_diag = here_row == here_col % grid_rows
    tri = jnp.arange(block)[:, None] >= jnp.arange(block)[None, :]
    for u in range(col_blocks):
        top = u * ratio + here_col // grid_rows
        own_tile = lax.dynamic_slice(tiles, (top, u, 0, 0), (1, 1, block, block))[0, 0]
        sym_tile = jnp.where(tri, own_tile, own_tile.T)
        old_tile = lax.dynamic_slice(base, (top, u, 0, 0), (1, 1, block, block))[0, 0]
        new_tile = jnp.where(on_diag, sym_tile, old_tile)
        base = lax.dynamic_update_slice(base, new_tile[None, None], (top, u, 0, 0))
    base = jnp.transpose(base, (0, 2, 1, 3)).reshape(height, width)
    base, assembled = lax.optimization_barrier((base, assembled))
    def solve(rows):
        first = jnp.dot(rows[:, :block], inv00.T, precision=HIGH)
        second = jnp.dot(
            rows[:, block:] - jnp.dot(first, f10.T, precision=HIGH), inv11.T, precision=HIGH
        )
        return jnp.concatenate([first, second], 1)

    head_first = jnp.where(here_row == 0, f00, f10)
    head_second = jnp.where(here_row == 0, jnp.zeros_like(f11), f11)
    head = jnp.concatenate([head_first, head_second], 1)
    offset = here_col // grid_rows
    chosen = lax.dynamic_index_in_dim(
        assembled.reshape(col_blocks, ratio, block, 2 * block), offset, 1, keepdims=False
    )
    picked = solve(chosen.reshape(width, 2 * block)).reshape(col_blocks, block, 2 * block)
    picked = picked.at[0].set(jnp.where((here_row < 2) & (offset == 0), head, picked[0]))
    pairs = []
    for g in range(grid_rows):
        for s in range(grid_cols):
            dst_row = s % grid_rows
            dst_col = g + grid_rows * (s // grid_rows)
            pairs.append((g * grid_cols + s, dst_row * grid_cols + dst_col))
    across = lax.ppermute(picked, ("row", "col"), pairs)

    panel = solve(assembled)
    panel = panel.at[:block].set(jnp.where(here_row < 2, head, panel[:block]))

    right = across.reshape(width, 2 * block)
    update = jnp.dot(panel, right.T, precision=lax.Precision.HIGH)
    full_i = jnp.repeat(block_i, block)[:, None]
    full_j = jnp.repeat(block_j, block)[None, :]
    result = base - jnp.where(full_i >= full_j, update, 0.0)
    panel_col = lax.dynamic_slice_in_dim(panel, jnp.minimum(here_col, 1) * block, block, 1)
    result = result.at[:, :block].set(jnp.where(here_col < 2, panel_col, result[:, :block]))
    return result.reshape(row_blocks, 1, block, col_blocks, 1, block)


def solution(mesh):
    return jax.shard_map(
        shards,
        mesh=mesh,
        in_specs=(
            P(None, "row", None, None, "col", None),
            P(("row", "col"), None, None, None),
            P(("row", "col"), None, None),
            P(("row", "col"), None),
            P(("row", "col")),
            P(),
        ),
        out_specs=P(None, "row", None, None, "col", None),
        check_vma=False,
    )
```

```python
import jax
import jax.numpy as jnp
from jax import lax
from jax.sharding import PartitionSpec as P

HIGH = lax.Precision.HIGHEST


def symmetric(block):
    return jnp.tril(block) + jnp.swapaxes(jnp.tril(block, -1), -1, -2)


def lower_inverse(lower_factor):
    ident = jnp.eye(lower_factor.shape[0], dtype=lower_factor.dtype)
    return jax.scipy.linalg.solve_triangular(lower_factor, ident, lower=True)


def leading(block00, block10, block11, link):
    size = block00.shape[0]
    first = symmetric(block00)
    second = symmetric(block11)
    coupled = link * block10
    whole = jnp.concatenate(
        [jnp.concatenate([first, coupled.T], 1), jnp.concatenate([coupled, second], 1)], 0
    )
    ident = jnp.eye(2 * size, dtype=whole.dtype)
    spread = jnp.sum(jnp.abs(whole), axis=1) - jnp.abs(jnp.diagonal(whole))
    whole = whole * (1.0 - ident) + ident * (1.0 + spread)[:, None]
    factor00 = jnp.linalg.cholesky(whole[:size, :size])
    inv00 = lower_inverse(factor00)
    factor10 = jnp.dot(whole[size:, :size], inv00.T, precision=HIGH)
    reduced = whole[size:, size:] - jnp.dot(factor10, factor10.T, precision=HIGH)
    factor11 = jnp.linalg.cholesky(reduced)
    inv11 = lower_inverse(factor11)
    return factor00, factor10, factor11, inv00, inv11


def shards(hess, coupling, dest_row, local_row, live, pattern):
    grid_rows = lax.axis_size("row")
    grid_cols = lax.axis_size("col")
    here_row = lax.axis_index("row")
    here_col = lax.axis_index("col")
    row_blocks = hess.shape[0]
    col_blocks = hess.shape[3]
    block = hess.shape[2]
    slot_count = coupling.shape[1]
    bucket = slot_count // 4
    height = row_blocks * block
    width = col_blocks * block
    ratio = grid_cols // grid_rows
    mask = pattern.astype(jnp.float32)

    corner = hess[0, 0, :, 0, 0, :].astype(jnp.float32)
    devices = grid_rows * grid_cols
    here = here_row * grid_cols + here_col
    pivots = []
    for source in (0, grid_cols, grid_cols + 1):
        value = jnp.where(here == source, corner, 0.0)
        reach = 1
        while reach < devices:
            pairs = [
                ((source + m) % devices, (source + m + reach) % devices)
                for m in range(min(reach, devices - reach))
            ]
            value = value + lax.ppermute(value, ("row", "col"), pairs)
            reach *= 2
        pivots.append(value)

    grid_ids = jnp.arange(grid_rows, dtype=jnp.int32)
    dest = dest_row[0, :, 0]
    active = jnp.arange(slot_count, dtype=jnp.int32) < live[0]
    hits = (dest[:, None] == grid_ids[None, :]) & active[:, None]
    ranks = jnp.cumsum(hits.astype(jnp.int32), axis=0) - 1
    place = jnp.sum(jnp.where(hits, ranks + grid_ids[None, :] * bucket, 0), axis=1)
    place = jnp.where(active, place, -1)
    pick = jnp.arange(grid_rows * bucket, dtype=jnp.int32)[:, None] == place[None, :]
    outgoing = jnp.dot(
        pick.astype(jnp.float32), coupling[0].reshape(slot_count, 2 * block), precision=HIGH
    )
    labels = jnp.sum(jnp.where(pick, local_row[0][None, :], 0), axis=1).astype(jnp.float32)
    tags = jnp.zeros((grid_rows * bucket, 128), jnp.float32).at[:, 0].set(labels)
    combined = lax.all_to_all(
        jnp.concatenate([outgoing, tags], 1).reshape(grid_rows, bucket, 2 * block + 128),
        "row",
        split_axis=0,
        concat_axis=0,
        tiled=True,
    ).reshape(grid_rows * bucket, 2 * block + 128)
    arrived = combined[:, : 2 * block]
    spots = combined[:, 2 * block].astype(jnp.int32)
    spread = jnp.arange(height, dtype=jnp.int32)[:, None] == spots[None, :]
    partial_value = jnp.dot(
        spread.astype(jnp.float32), arrived.reshape(-1, 2 * block), precision=HIGH
    )
    own = hess[:, 0, :, 0, 0, :].astype(jnp.float32).reshape(height, block)
    which = (jnp.arange(2, dtype=jnp.int32) == here_col).astype(jnp.float32)
    which = jnp.repeat(which, block)
    partial_value = partial_value + jnp.concatenate([own, own], 1) * which[None, :]

    mine = lax.dynamic_index_in_dim(
        mask.reshape(row_blocks, grid_rows, -1), here_row, 1, keepdims=False
    )
    rowmask = jnp.repeat(jnp.repeat(mine[:, :2], block, axis=0), block, axis=1)
    assembled = lax.psum(partial_value * rowmask, "col")
    f00, f10, f11, inv00, inv11 = leading(pivots[0], pivots[1], pivots[2], mask[1, 0])
    late_hess, inv11 = lax.optimization_barrier((hess, inv11))
    tiles = jnp.transpose(late_hess[:, 0, :, :, 0, :], (0, 2, 1, 3)).astype(jnp.float32)
    block_i = jnp.arange(row_blocks, dtype=jnp.int32) * grid_rows + here_row
    block_j = jnp.arange(col_blocks, dtype=jnp.int32) * grid_cols + here_col
    links = lax.dynamic_index_in_dim(
        lax.dynamic_index_in_dim(
            mask.reshape(row_blocks, grid_rows, col_blocks, grid_cols), here_row, 1, keepdims=False
        ),
        here_col,
        2,
        keepdims=False,
    )
    below = (block_i[:, None] > block_j[None, :])[:, :, None, None]
    base = jnp.where(below, links[:, :, None, None] * tiles, 0.0)
    on_diag = here_row == here_col % grid_rows
    tri = jnp.arange(block)[:, None] >= jnp.arange(block)[None, :]
    for u in range(col_blocks):
        top = u * ratio + here_col // grid_rows
        own_tile = lax.dynamic_slice(tiles, (top, u, 0, 0), (1, 1, block, block))[0, 0]
        sym_tile = jnp.where(tri, own_tile, own_tile.T)
        old_tile = lax.dynamic_slice(base, (top, u, 0, 0), (1, 1, block, block))[0, 0]
        new_tile = jnp.where(on_diag, sym_tile, old_tile)
        base = lax.dynamic_update_slice(base, new_tile[None, None], (top, u, 0, 0))
    base = jnp.transpose(base, (0, 2, 1, 3)).reshape(height, width)
    base, assembled = lax.optimization_barrier((base, assembled))
    def solve(rows):
        first = jnp.dot(rows[:, :block], inv00.T, precision=HIGH)
        second = jnp.dot(
            rows[:, block:] - jnp.dot(first, f10.T, precision=HIGH), inv11.T, precision=HIGH
        )
        return jnp.concatenate([first, second], 1)

    head_first = jnp.where(here_row == 0, f00, f10)
    head_second = jnp.where(here_row == 0, jnp.zeros_like(f11), f11)
    head = jnp.concatenate([head_first, head_second], 1)
    offset = here_col // grid_rows
    chosen = lax.dynamic_index_in_dim(
        assembled.reshape(col_blocks, ratio, block, 2 * block), offset, 1, keepdims=False
    )
    picked = solve(chosen.reshape(width, 2 * block)).reshape(col_blocks, block, 2 * block)
    picked = picked.at[0].set(jnp.where((here_row < 2) & (offset == 0), head, picked[0]))
    pairs = []
    for g in range(grid_rows):
        for s in range(grid_cols):
            dst_row = s % grid_rows
            dst_col = g + grid_rows * (s // grid_rows)
            pairs.append((g * grid_cols + s, dst_row * grid_cols + dst_col))
    across = lax.ppermute(picked, ("row", "col"), pairs)

    panel = solve(assembled)
    panel = panel.at[:block].set(jnp.where(here_row < 2, head, panel[:block]))

    right = across.reshape(width, 2 * block)
    update = jnp.dot(panel, right.T, precision=lax.Precision.HIGH)
    full_i = jnp.repeat(block_i, block)[:, None]
    full_j = jnp.repeat(block_j, block)[None, :]
    result = base - jnp.where(full_i >= full_j, update, 0.0)
    panel_col = lax.dynamic_slice_in_dim(panel, jnp.minimum(here_col, 1) * block, block, 1)
    result = result.at[:, :block].set(jnp.where(here_col < 2, panel_col, result[:, :block]))
    return result.reshape(row_blocks, 1, block, col_blocks, 1, block)


def solution(mesh):
    return jax.shard_map(
        shards,
        mesh=mesh,
        in_specs=(
            P(None, "row", None, None, "col", None),
            P(("row", "col"), None, None, None),
            P(("row", "col"), None, None),
            P(("row", "col"), None),
            P(("row", "col")),
            P(),
        ),
        out_specs=P(None, "row", None, None, "col", None),
        check_vma=False,
    )
```
